512 devices in a mesh: grp: 16 (over z), ep: 32 (over x, y, core).
Axes of the slice: x: 4, y: 4, z: 16, core: 2. Of those that a mesh axis runs over, the one named last changes fastest.
Arguments:
- q_nope: bfloat16 [3072, 2048], P(('grp', 'ep')), may hold values from -15 to 15
- q_rope: bfloat16 [3072, 1024], P(('grp', 'ep')), may hold values from -8 to 8
- tree_latent: bfloat16 [3072, 576], P(('grp', 'ep')), may hold values from -12 to 12
- cache_pool: bfloat16 [4096, 64, 576], P(('grp', 'ep')), may hold values from -7 to 7
- page_table: int32 [4096], P(('grp', 'ep')), may hold values from 0 to 7, as said below
- cache_len: int32 [64], P('grp'), may hold values from 512 to 4096
- parents: int32 [64, 48], P('grp'), may hold values from 0 to 46, as said below
- w_key: bfloat16 [16, 512, 128], replicated, may hold values from -0.5 to 0.5
- w_value: bfloat16 [16, 512, 128], P('grp'), may hold values from -0.25 to 0.25
- out_weight: bfloat16 [2048, 2048], P('grp'), may hold values from -0.125 to 0.125
Outputs:
- attn_out: bfloat16 [3072, 2048], P(('grp', 'ep'))
The draws below stay inside these ranges and needn't reach their ends.
Inputs may be any that keep to these rules, and one draw needn't show every extreme that they name: `page_table`: each device's block of 8 entries is an arrangement of 0 to 7; entry k of the block names the page of that device's own block of the pool that holds the device's k-th page of positions. parents[r, 0] = 0, and for i >= 1, max(0, i - 4) <= parents[r, i] <= i - 1.
All inputs are finite; a program needn't handle non-finite values.
Results may differ from the reference program's by a relative error of at most 0.039.
Values may be sent and summed in bfloat16 or wider, within the bound.
No kernel may reach another device: no remote copies, remote signals or barrier semaphores. Data moves between devices by JAX's collectives and lax.ppermute only.
A program may use at most 64 MiB of HBM per device.

```python
import math
import jax
import jax.numpy as jnp
from jax import lax

D = 2048
HEADS = 16
NOPE = 128
ROPE = 64
RANK = 512
TREE = 48
PAGE = 64
POS_DEV = 512
LAT = 576
DEV_REQ = 8
REQS = 64
TOKENS = 3072
MAXLEN = 4096
PAGES_DEV = 8
POOL = 4096


def slot_table(key):
    blocks = POOL // PAGES_DEV
    draws = jax.random.randint(jax.random.fold_in(key, 11), (blocks, PAGES_DEV), 0, 65536)
    ranked = draws * PAGES_DEV + jnp.arange(PAGES_DEV, dtype=jnp.int32)[None, :]
    return jnp.argsort(ranked, axis=1).astype(jnp.int32)


def draw_page_table(key, part):
    return slot_table(key).reshape(POOL)


def draw_cache_pool(key, part):
    shape = (POOL, PAGE, LAT)
    values = jnp.clip(jax.random.normal(jax.random.fold_in(key, 21), shape, jnp.float32), -6.0, 6.0)
    return values.astype(jnp.bfloat16)


def draw_q_rope(key, part):
    shape = (TOKENS, HEADS * ROPE)
    values = jnp.clip(jax.random.normal(jax.random.fold_in(key, 27), shape, jnp.float32), -6.0, 6.0)
    return values.astype(jnp.bfloat16)


def draw_cache_len(key, part):
    lengths = jax.random.randint(jax.random.fold_in(key, 31), (REQS,), MAXLEN // 8, MAXLEN + 1)
    longest = jax.random.randint(jax.random.fold_in(key, 33), (), 0, REQS)
    offset = jax.random.randint(jax.random.fold_in(key, 35), (), 0, REQS - 1)
    shortest = (longest + 1 + offset) % REQS
    lengths = lengths.at[longest].set(MAXLEN)
    lengths = lengths.at[shortest].set(MAXLEN // 8)
    return lengths.astype(jnp.int32)


def draw_parents(key, part):
    order = jnp.arange(TREE, dtype=jnp.int32)
    draws = jax.random.randint(jax.random.fold_in(key, 41), (REQS, TREE), 0, 65536)
    spread = jnp.maximum(jnp.minimum(order, 4), 1)
    offset = draws % spread[None, :]
    chosen = jnp.where(order[None, :] > 0, order[None, :] - 1 - offset, 0)
    return chosen.astype(jnp.int32)


def steps_of(own_key, shape, split, smallest, largest):
    factor_of, own = 1.0, jax.random.fold_in(own_key, 6)
    for axis_at, shards_of in split:
        steps = jnp.exp(jax.random.uniform(jax.random.fold_in(own, axis_at), (shards_of,), jnp.float32, smallest / len(split), largest / len(split)))
        factor_of = factor_of * jnp.repeat(steps, shape[axis_at] // shards_of).reshape([-1 if axis == axis_at else 1 for axis in range(len(shape))])
    return factor_of


def noise(key, shape, deviation, most, cuts=(), kind=jnp.bfloat16):
    result = jax.random.normal(key, shape, jnp.float32) * deviation
    if len(cuts) > 0:
        result = steps_of(key, shape, cuts, -0.22, 0.18) * result
    return jnp.clip(result, min=-most, max=most).astype(kind)


def setup_inputs(seed: int = 0) -> dict:
    key_of = jax.random.split(jax.random.key(seed), 11)
    return {
        "q_nope": noise(key_of[0], (TOKENS, HEADS * NOPE), 2.5, 15.0, ((0, 512),)),
        "q_rope": draw_q_rope(jax.random.fold_in(key_of[10], 71), 0),
        "tree_latent": noise(key_of[2], (TOKENS, LAT), 2.0, 12.0, ((0, 512),)),
        "cache_pool": draw_cache_pool(jax.random.fold_in(key_of[10], 71), 0),
        "page_table": draw_page_table(jax.random.fold_in(key_of[10], 71), 0),
        "cache_len": draw_cache_len(jax.random.fold_in(key_of[10], 71), 0),
        "parents": draw_parents(jax.random.fold_in(key_of[10], 71), 0),
        "w_key": noise(key_of[7], (HEADS, RANK, NOPE), NOPE ** -0.5, 0.5),
        "w_value": noise(key_of[8], (HEADS, RANK, NOPE), RANK ** -0.5, 0.25, ((0, 16),)),
        "out_weight": noise(key_of[9], (HEADS * NOPE, D), (HEADS * NOPE) ** -0.5, 0.125, ((0, 16),)),
    }


def ancestors(parent_row):
    count = parent_row.shape[0]
    order = jnp.arange(count, dtype=jnp.int32)
    links = ((order[None, :] == parent_row[:, None]) & (order[:, None] > 0)).astype(jnp.float32)
    reach = jnp.eye(count, dtype=jnp.float32) + links
    for repeat in range(int(count).bit_length()):
        reach = jnp.minimum(jnp.dot(reach, reach, precision=lax.Precision.HIGHEST), 1.0)
    return reach > 0.5

def reference(q_nope, q_rope, tree_latent, cache_pool, page_table, cache_len, parents, w_key, w_value, out_weight):
    nope_rows = q_nope.reshape(TOKENS, HEADS, NOPE).astype(jnp.float32)
    absorbed = jnp.einsum('thn,hrn->thr', nope_rows, w_key.astype(jnp.float32)).astype(jnp.bfloat16)
    queries = jnp.concatenate([absorbed, q_rope.reshape(TOKENS, HEADS, ROPE)], axis=2)
    score_scale = 1.0 / math.sqrt(NOPE + ROPE)
    places = jnp.arange(MAXLEN, dtype=jnp.int32)

    def one_request(request):
        holder = request * DEV_REQ + places // POS_DEV
        logical = holder * PAGES_DEV + places % POS_DEV // PAGE
        physical = holder * PAGES_DEV + page_table[logical]
        cached = cache_pool[physical, places % PAGE]
        fresh = lax.dynamic_slice_in_dim(tree_latent, (request * TREE).astype(jnp.int32), TREE, 0)
        all_keys = jnp.concatenate([cached, fresh], axis=0).astype(jnp.float32)
        own_queries = lax.dynamic_slice_in_dim(queries, (request * TREE).astype(jnp.int32), TREE, 0).astype(jnp.float32)
        scores = jnp.einsum('ihl,kl->ihk', own_queries, all_keys) * score_scale
        cache_ok = places < cache_len[request]
        family = ancestors(parents[request])
        allowed = jnp.concatenate([jnp.broadcast_to(cache_ok[None, :], (TREE, MAXLEN)), family], axis=1)
        masked = jnp.where(allowed[:, None, :], scores, -jnp.inf)
        highest = lax.optimization_barrier(jnp.max(masked, axis=2, keepdims=True))
        powers = jnp.exp(masked - highest)
        weights = (powers / lax.optimization_barrier(jnp.sum(powers, axis=2, keepdims=True))).astype(jnp.bfloat16)
        latent = jnp.einsum('ihk,kr->ihr', weights.astype(jnp.float32), all_keys[:, :RANK])
        return latent
    latent = lax.map(one_request, jnp.arange(REQS, dtype=jnp.int32)).reshape(TOKENS, HEADS, RANK)
    head_rows = jnp.einsum('thr,hrn->thn', latent, w_value.astype(jnp.float32), precision=lax.Precision.HIGHEST)
    head_rows = head_rows.astype(jnp.bfloat16).reshape(TOKENS, HEADS * NOPE)
    return jnp.dot(head_rows, out_weight, preferred_element_type=jnp.float32).astype(jnp.bfloat16)
```

```python
import math

import jax
import jax.numpy as jnp
from jax import lax
from jax.sharding import PartitionSpec as P

REQ_GRP = 4


def shifted(block, axis, group, shift):
    count = lax.axis_size(axis)
    route = [(i, (i // group) * group + (i % group + shift) % group) for i in range(count)]
    return lax.ppermute(block, axis, route)


def ancestors(parent_row):
    count = parent_row.shape[0]
    order = jnp.arange(count, dtype=jnp.int32)
    links = ((order[None, :] == parent_row[:, None]) & (order[:, None] > 0)).astype(jnp.float32)
    reach = jnp.eye(count, dtype=jnp.float32) + links
    for repeat in range(int(count).bit_length()):
        reach = jnp.minimum(jnp.dot(reach, reach, precision=lax.Precision.HIGHEST), 1.0)
    return reach > 0.5


def absorb(nope_rows, w_key):
    return jnp.einsum("thn,hrn->thr", nope_rows, w_key, preferred_element_type=jnp.float32).astype(
        jnp.bfloat16
    )


def per_device(
    q_nope,
    q_rope,
    tree_latent,
    cache_pool,
    page_table,
    cache_len,
    parents,
    w_key,
    w_value,
    out_weight,
):
    head_count = w_key.shape[0]
    latent_width = w_key.shape[1]
    nope_width = w_key.shape[2]
    token_count = q_nope.shape[0]
    rope_width = q_rope.shape[1] // head_count
    ep_size = lax.axis_size("ep")
    grp_size = lax.axis_size("grp")
    per_request = ep_size // REQ_GRP
    position = lax.axis_index("ep")
    local_rank = position % per_request
    local_request = position // per_request
    score_scale = 1.0 / math.sqrt(nope_width + rope_width)

    nope_rows = q_nope.reshape(token_count, head_count, nope_width)
    rope_rows = q_rope.reshape(token_count, head_count, rope_width)
    queries = jnp.concatenate([absorb(nope_rows, w_key), rope_rows], axis=2)
    blocks = [queries] + [
        shifted(queries, "ep", per_request, s) for s in range(1, per_request)
    ]
    all_queries = jnp.concatenate(blocks, axis=0)

    page_count, page_rows, key_width = cache_pool.shape
    cached = cache_pool.reshape(page_count * page_rows, key_width)
    pos_count = cached.shape[0]
    all_keys = jnp.concatenate([cached, tree_latent], axis=0)
    slots = jnp.arange(page_count, dtype=jnp.int32)
    logical_of_slot = jnp.sum(
        jnp.where(page_table[:, None] == slots[None, :], slots[:, None], 0), axis=0
    )
    place = (
        local_rank * pos_count
        + jnp.repeat(logical_of_slot, page_rows) * page_rows
        + jnp.tile(jnp.arange(page_rows, dtype=jnp.int32), page_count)
    )
    my_length = lax.dynamic_index_in_dim(cache_len, local_request, 0, keepdims=False)
    cache_ok = place < my_length
    parent_row = lax.dynamic_index_in_dim(parents, local_request, 0, keepdims=False)
    family = ancestors(parent_row)
    tree_cols = lax.dynamic_slice_in_dim(family, local_rank * token_count, token_count, 1)
    source_rank = (local_rank - jnp.arange(per_request, dtype=jnp.int32)) % per_request
    tree_ok = jnp.take(
        tree_cols.reshape(per_request, token_count, token_count), source_rank, axis=0
    ).reshape(per_request * token_count, token_count)
    query_count = per_request * token_count
    allowed = jnp.concatenate(
        [jnp.broadcast_to(cache_ok[None, :], (query_count, pos_count)), tree_ok], axis=1
    )
    scores = (
        jnp.einsum("ihl,kl->ihk", all_queries, all_keys, preferred_element_type=jnp.float32)
        * score_scale
    )
    masked = jnp.where(allowed[:, None, :], scores, -1e30)
    highest = jnp.max(masked, axis=2)
    high_hi = highest.astype(jnp.bfloat16)
    high_lo = (highest - high_hi.astype(jnp.float32)).astype(jnp.bfloat16)
    sent_high = high_hi.astype(jnp.float32) + high_lo.astype(jnp.float32)
    powers = jnp.where(allowed[:, None, :], jnp.exp(masked - sent_high[..., None]), 0.0)
    total = jnp.sum(powers, axis=2)
    partial_value = jnp.einsum(
        "ihk,kr->ihr",
        powers.astype(jnp.bfloat16),
        all_keys[:, :latent_width],
        preferred_element_type=jnp.float32,
    ).astype(jnp.bfloat16)
    stats = jnp.stack([high_hi, high_lo, total.astype(jnp.bfloat16)], axis=0)
    part_blocks = partial_value.reshape(per_request, token_count, head_count, latent_width)
    stat_blocks = stats.reshape(3, per_request, token_count, head_count)
    got_values = [part_blocks[0]]
    got_stats = [stat_blocks[:, 0]]
    for s in range(1, per_request):
        got_values.append(shifted(part_blocks[s], "ep", per_request, per_request - s))
        got_stats.append(shifted(stat_blocks[:, s], "ep", per_request, per_request - s))
    got_stats = jnp.stack(got_stats, axis=0).astype(jnp.float32)
    got_high = got_stats[:, 0] + got_stats[:, 1]
    joint_high = jnp.max(got_high, axis=0)
    factors = jnp.exp(got_high - joint_high[None])
    merged_total = jnp.sum(got_stats[:, 2] * factors, axis=0)
    merged_sum = sum(
        got_values[s].astype(jnp.float32) * factors[s][..., None] for s in range(per_request)
    )
    merged = (merged_sum / merged_total[..., None]).astype(jnp.bfloat16)

    group = lax.axis_index("grp")
    by_head = jnp.take(
        jnp.swapaxes(merged, 0, 1),
        (group + jnp.arange(grp_size, dtype=jnp.int32)) % grp_size,
        axis=0,
    )
    spread = [by_head[0]] + [shifted(by_head[s], "grp", grp_size, s) for s in range(1, grp_size)]
    spread = jnp.concatenate(spread, axis=0)
    head_rows = jnp.dot(spread, w_value[0], preferred_element_type=jnp.float32).astype(jnp.bfloat16)
    partial_out = jnp.dot(head_rows, out_weight, preferred_element_type=jnp.float32).astype(
        jnp.bfloat16
    )
    partial_out = partial_out.reshape(grp_size, token_count, partial_out.shape[1])
    result = partial_out[0].astype(jnp.float32)
    for s in range(1, grp_size):
        result = result + shifted(partial_out[s], "grp", grp_size, grp_size - s).astype(jnp.float32)
    return result.astype(jnp.bfloat16)


def solution(mesh):
    return jax.shard_map(
        per_device,
        mesh=mesh,
        in_specs=(
            P(("grp", "ep"), None),
            P(("grp", "ep"), None),
            P(("grp", "ep"), None),
            P(("grp", "ep"), None, None),
            P(("grp", "ep")),
            P("grp"),
            P("grp", None),
            P(),
            P("grp", None, None),
            P("grp", None),
        ),
        out_specs=P(("grp", "ep"), None),
        check_vma=False,
    )
```

```python
import math

import jax
import jax.numpy as jnp
from jax import lax
from jax.sharding import PartitionSpec as P

TREE = 48
REQ_GRP = 4


def from_partner(block, axis, bit):
    count = lax.axis_size(axis)
    route = []
    for low in range(count):
        high = low | 1 << bit
        if high != low and high < count:
            route += [(low, high), (high, low)]
    return lax.ppermute(block, axis, route)


def bit_reversed(count):
    width = count.bit_length() - 1
    return [int(format(index, f"0{width}b")[::-1], 2) if width else 0 for index in range(count)]


def ancestors(parent_row):
    count = parent_row.shape[0]
    order = jnp.arange(count, dtype=jnp.int32)
    links = ((order[None, :] == parent_row[:, None]) & (order[:, None] > 0)).astype(jnp.float32)
    reach = jnp.eye(count, dtype=jnp.float32) + links
    for repeat in range(int(count).bit_length()):
        reach = jnp.minimum(jnp.dot(reach, reach, precision=lax.Precision.HIGHEST), 1.0)
    return reach > 0.5


def absorb(nope_rows, w_key):
    return jnp.einsum("thn,hrn->thr", nope_rows, w_key, preferred_element_type=jnp.float32).astype(
        jnp.bfloat16
    )


def append_partner(mine, partner, position, bit_level):
    upper_side = jnp.right_shift(position, bit_level) & 1 == 1
    former = jnp.where(upper_side, partner, mine)
    latter = jnp.where(upper_side, mine, partner)
    return jnp.concatenate([former, latter], axis=0)


def split_high(high):
    high_hi = high.astype(jnp.bfloat16)
    high_lo = (high - high_hi.astype(jnp.float32)).astype(jnp.bfloat16)
    return high_hi, high_lo


def pack_part(part_sum, part_high, part_total, width):
    high_hi, high_lo = split_high(part_high)
    stats = jnp.concatenate([high_hi, high_lo, part_total.astype(jnp.bfloat16)], axis=1)
    stats = jnp.pad(stats, ((0, 0), (0, width - stats.shape[1])))
    return jnp.concatenate([part_sum.astype(jnp.bfloat16), stats[:, None, :]], axis=1)


def unpack_part(packed, heads):
    stats = packed[:, heads].astype(jnp.float32)
    high = stats[:, :heads] + stats[:, heads : 2 * heads]
    total = stats[:, 2 * heads : 3 * heads]
    return packed[:, :heads].astype(jnp.float32), high, total


def combine_parts(kept_part, received):
    kept_sum, kept_high, kept_total = kept_part
    got_sum, got_high, got_total = received
    joint_high = jnp.maximum(kept_high, got_high)
    factor_kept = jnp.exp(kept_high - joint_high)
    factor_got = jnp.exp(got_high - joint_high)
    merged_sum = kept_sum * factor_kept[..., None] + got_sum * factor_got[..., None]
    merged_total = kept_total * factor_kept + got_total * factor_got
    return (merged_sum, joint_high, merged_total)


def per_device(
    q_nope,
    q_rope,
    tree_latent,
    cache_pool,
    page_table,
    cache_len,
    parents,
    w_key,
    w_value,
    out_weight,
):
    head_count = w_key.shape[0]
    latent_width = w_key.shape[1]
    nope_width = w_key.shape[2]
    token_count = q_nope.shape[0]
    rope_width = q_rope.shape[1] // head_count
    per_request = lax.axis_size("ep") // REQ_GRP
    grp_size = lax.axis_size("grp")
    doublings = per_request.bit_length() - 1
    position = lax.axis_index("ep")
    local_rank = position % per_request
    local_request = position // per_request
    score_scale = 1.0 / math.sqrt(nope_width + rope_width)
    nope_rows = q_nope.reshape(token_count, head_count, nope_width)
    rope_rows = q_rope.reshape(token_count, head_count, rope_width)
    queries = jnp.concatenate([absorb(nope_rows, w_key), rope_rows], axis=2)
    for bit_level in reversed(range(doublings)):
        partner = from_partner(queries, "ep", bit_level)
        queries = append_partner(queries, partner, position, bit_level)
    cached = cache_pool.reshape(-1, cache_pool.shape[2])
    page_count, page_rows = cache_pool.shape[0], cache_pool.shape[1]
    pos_count = cached.shape[0]
    all_keys = jnp.concatenate([cached, tree_latent], axis=0)
    slots = jnp.arange(page_count, dtype=jnp.int32)
    logical_of_slot = jnp.sum(
        jnp.where(page_table[:, None] == slots[None, :], slots[:, None], 0), axis=0
    )
    place = (
        local_rank * pos_count
        + jnp.repeat(logical_of_slot, page_rows) * page_rows
        + jnp.tile(jnp.arange(page_rows, dtype=jnp.int32), page_count)
    )
    my_length = lax.dynamic_index_in_dim(cache_len, local_request, 0, keepdims=False)
    cache_ok = place < my_length
    parent_row = lax.dynamic_index_in_dim(parents, local_request, 0, keepdims=False)
    family = ancestors(parent_row)
    tree_cols = lax.dynamic_slice_in_dim(family, local_rank * token_count, token_count, 1)
    tree_ok = tree_cols.reshape(per_request, token_count, token_count)[
        jnp.array(bit_reversed(per_request))
    ].reshape(TREE, token_count)
    allowed = jnp.concatenate(
        [jnp.broadcast_to(cache_ok[None, :], (TREE, pos_count)), tree_ok], axis=1
    )
    scores = (
        jnp.einsum("ihl,kl->ihk", queries, all_keys, preferred_element_type=jnp.float32)
        * score_scale
    )
    masked = jnp.where(allowed[:, None, :], scores, -1e30)
    highest = jnp.max(masked, axis=2)
    powers = jnp.where(allowed[:, None, :], jnp.exp(masked - highest[..., None]), 0.0)
    total = jnp.sum(powers, axis=2)
    partial_value = jnp.einsum(
        "ihk,kr->ihr",
        powers.astype(jnp.bfloat16),
        all_keys[:, :latent_width],
        preferred_element_type=jnp.float32,
    )
    state = (partial_value, highest, total)
    for bit_level in range(doublings):
        half_rows = state[0].shape[0] // 2
        upper_side = jnp.right_shift(position, bit_level) & 1 == 1
        lower_part = tuple((member[:half_rows] for member in state))
        upper_part = tuple((member[half_rows:] for member in state))
        kept_part = tuple(
            (jnp.where(upper_side, upper, lower) for lower, upper in zip(lower_part, upper_part))
        )
        sent_part = tuple(
            (jnp.where(upper_side, lower, upper) for lower, upper in zip(lower_part, upper_part))
        )
        received = from_partner(pack_part(*sent_part, latent_width), "ep", bit_level)
        state = combine_parts(kept_part, unpack_part(received, head_count))
    merged_sum, merged_high, merged_total = state
    merged = merged_sum / merged_total[..., None]
    spread = lax.all_to_all(
        merged.astype(jnp.bfloat16), "grp", split_axis=1, concat_axis=0, tiled=True
    )
    spread = spread.reshape(grp_size, token_count, latent_width)[jnp.array(bit_reversed(grp_size))]
    head_rows = jnp.dot(
        spread.reshape(grp_size * token_count, latent_width),
        w_value[0],
        preferred_element_type=jnp.float32,
    ).astype(jnp.bfloat16)
    rows_out = jnp.dot(head_rows, out_weight, preferred_element_type=jnp.float32)
    group = lax.axis_index("grp")
    for bit_level in range(grp_size.bit_length() - 1):
        half_rows = rows_out.shape[0] // 2
        upper_side = jnp.right_shift(group, bit_level) & 1 == 1
        lower, upper = rows_out[:half_rows], rows_out[half_rows:]
        kept = jnp.where(upper_side, upper, lower)
        sent = jnp.where(upper_side, lower, upper)
        rows_out = kept + from_partner(sent.astype(jnp.bfloat16), "grp", bit_level).astype(
            jnp.float32
        )
    return rows_out.astype(jnp.bfloat16)


def solution(mesh):
    return jax.shard_map(
        per_device,
        mesh=mesh,
        in_specs=(
            P(("grp", "ep"), None),
            P(("grp", "ep"), None),
            P(("grp", "ep"), None),
            P(("grp", "ep"), None, None),
            P(("grp", "ep")),
            P("grp"),
            P("grp", None),
            P(),
            P("grp", None, None),
            P("grp", None),
        ),
        out_specs=P(("grp", "ep"), None),
        check_vma=False,
    )
```

```python
import math

import jax
import jax.numpy as jnp
from jax import lax
from jax.sharding import PartitionSpec as P

TREE = 48
REQ_GRP = 4


def from_partner(block, axis, bit):
    count = lax.axis_size(axis)
    route = []
    for low in range(count):
        high = low | 1 << bit
        if high != low and high < count:
            route += [(low, high), (high, low)]
    return lax.ppermute(block, axis, route)


def bit_reversed(count):
    width = count.bit_length() - 1
    return [int(format(index, f"0{width}b")[::-1], 2) if width else 0 for index in range(count)]


def ancestors(parent_row):
    count = parent_row.shape[0]
    order = jnp.arange(count, dtype=jnp.int32)
    links = ((order[None, :] == parent_row[:, None]) & (order[:, None] > 0)).astype(jnp.float32)
    reach = jnp.eye(count, dtype=jnp.float32) + links
    for repeat in range(int(count).bit_length()):
        reach = jnp.minimum(jnp.dot(reach, reach, precision=lax.Precision.HIGHEST), 1.0)
    return reach > 0.5


def absorb(nope_rows, w_key):
    return jnp.einsum("thn,hrn->thr", nope_rows, w_key, preferred_element_type=jnp.float32).astype(
        jnp.bfloat16
    )


def append_partner(mine, partner, position, bit_level):
    upper_side = jnp.right_shift(position, bit_level) & 1 == 1
    former = jnp.where(upper_side, partner, mine)
    latter = jnp.where(upper_side, mine, partner)
    return jnp.concatenate([former, latter], axis=0)


def split_high(high):
    high_hi = high.astype(jnp.bfloat16)
    high_lo = (high - high_hi.astype(jnp.float32)).astype(jnp.bfloat16)
    return high_hi, high_lo


def pack_part(part_sum, part_high, part_total, width):
    high_hi, high_lo = split_high(part_high)
    stats = jnp.concatenate([high_hi, high_lo, part_total.astype(jnp.bfloat16)], axis=1)
    stats = jnp.pad(stats, ((0, 0), (0, width - stats.shape[1])))
    return jnp.concatenate([part_sum.astype(jnp.bfloat16), stats[:, None, :]], axis=1)


def unpack_part(packed, heads):
    stats = packed[:, heads].astype(jnp.float32)
    high = stats[:, :heads] + stats[:, heads : 2 * heads]
    total = stats[:, 2 * heads : 3 * heads]
    return packed[:, :heads].astype(jnp.float32), high, total


def combine_parts(kept_part, received):
    kept_sum, kept_high, kept_total = kept_part
    got_sum, got_high, got_total = received
    joint_high = jnp.maximum(kept_high, got_high)
    factor_kept = jnp.exp(kept_high - joint_high)
    factor_got = jnp.exp(got_high - joint_high)
    merged_sum = kept_sum * factor_kept[..., None] + got_sum * factor_got[..., None]
    merged_total = kept_total * factor_kept + got_total * factor_got
    return (merged_sum, joint_high, merged_total)


def per_device(
    q_nope,
    q_rope,
    tree_latent,
    cache_pool,
    page_table,
    cache_len,
    parents,
    w_key,
    w_value,
    out_weight,
):
    head_count = w_key.shape[0]
    latent_width = w_key.shape[1]
    nope_width = w_key.shape[2]
    token_count = q_nope.shape[0]
    rope_width = q_rope.shape[1] // head_count
    per_request = lax.axis_size("ep") // REQ_GRP
    grp_size = lax.axis_size("grp")
    doublings = per_request.bit_length() - 1
    position = lax.axis_index("ep")
    local_rank = position % per_request
    local_request = position // per_request
    score_scale = 1.0 / math.sqrt(nope_width + rope_width)
    column_count = out_weight.shape[1] // 2
    own_columns = lax.dynamic_slice_in_dim(out_weight, (position & 1) * column_count, column_count, 1)
    out_columns = lax.all_gather(own_columns, "grp", axis=0, tiled=True)
    all_values = lax.all_gather(w_value, "grp", axis=0, tiled=True)
    nope_rows = q_nope.reshape(token_count, head_count, nope_width)
    rope_rows = q_rope.reshape(token_count, head_count, rope_width)
    queries = jnp.concatenate([absorb(nope_rows, w_key), rope_rows], axis=2)
    for bit_level in reversed(range(doublings)):
        partner = from_partner(queries, "ep", bit_level)
        queries = append_partner(queries, partner, position, bit_level)
    cached = cache_pool.reshape(-1, cache_pool.shape[2])
    page_count, page_rows = cache_pool.shape[0], cache_pool.shape[1]
    pos_count = cached.shape[0]
    all_keys = jnp.concatenate([cached, tree_latent], axis=0)
    slots = jnp.arange(page_count, dtype=jnp.int32)
    logical_of_slot = jnp.sum(
        jnp.where(page_table[:, None] == slots[None, :], slots[:, None], 0), axis=0
    )
    place = (
        local_rank * pos_count
        + jnp.repeat(logical_of_slot, page_rows) * page_rows
        + jnp.tile(jnp.arange(page_rows, dtype=jnp.int32), page_count)
    )
    my_length = lax.dynamic_index_in_dim(cache_len, local_request, 0, keepdims=False)
    cache_ok = place < my_length
    parent_row = lax.dynamic_index_in_dim(parents, local_request, 0, keepdims=False)
    family = ancestors(parent_row)
    tree_cols = lax.dynamic_slice_in_dim(family, local_rank * token_count, token_count, 1)
    tree_ok = tree_cols.reshape(per_request, token_count, token_count)[
        jnp.array(bit_reversed(per_request))
    ].reshape(TREE, token_count)
    allowed = jnp.concatenate(
        [jnp.broadcast_to(cache_ok[None, :], (TREE, pos_count)), tree_ok], axis=1
    )
    scores = (
        jnp.einsum("ihl,kl->ihk", queries, all_keys, preferred_element_type=jnp.float32)
        * score_scale
    )
    masked = jnp.where(allowed[:, None, :], scores, -1e30)
    highest = jnp.max(masked, axis=2)
    powers = jnp.where(allowed[:, None, :], jnp.exp(masked - highest[..., None]), 0.0)
    total = jnp.sum(powers, axis=2)
    partial_value = jnp.einsum(
        "ihk,kr->ihr",
        powers.astype(jnp.bfloat16),
        all_keys[:, :latent_width],
        preferred_element_type=jnp.float32,
    )
    state = (partial_value, highest, total)
    for bit_level in range(doublings):
        half_rows = state[0].shape[0] // 2
        upper_side = jnp.right_shift(position, bit_level) & 1 == 1
        lower_part = tuple((member[:half_rows] for member in state))
        upper_part = tuple((member[half_rows:] for member in state))
        kept_part = tuple(
            (jnp.where(upper_side, upper, lower) for lower, upper in zip(lower_part, upper_part))
        )
        sent_part = tuple(
            (jnp.where(upper_side, lower, upper) for lower, upper in zip(lower_part, upper_part))
        )
        received = from_partner(pack_part(*sent_part, latent_width), "ep", bit_level)
        state = combine_parts(kept_part, unpack_part(received, head_count))
    merged_sum, merged_high, merged_total = state
    merged = (merged_sum / merged_total[..., None]).astype(jnp.bfloat16)
    head_rows = jnp.einsum(
        "thr,hrn->thn", merged, all_values, preferred_element_type=jnp.float32
    ).astype(jnp.bfloat16)
    head_rows = head_rows.reshape(token_count, head_count * nope_width)
    both_rows = append_partner(head_rows, from_partner(head_rows, "ep", 0), position, 0)
    out_half = jnp.dot(both_rows, out_columns, preferred_element_type=jnp.float32).astype(
        jnp.bfloat16
    )
    core_upper = position & 1 == 1
    mine = jnp.where(core_upper, out_half[token_count:], out_half[:token_count])
    theirs = jnp.where(core_upper, out_half[:token_count], out_half[token_count:])
    other_half = from_partner(theirs, "ep", 0)
    return jnp.where(
        core_upper,
        jnp.concatenate([other_half, mine], axis=1),
        jnp.concatenate([mine, other_half], axis=1),
    )


def solution(mesh):
    return jax.shard_map(
        per_device,
        mesh=mesh,
        in_specs=(
            P(("grp", "ep"), None),
            P(("grp", "ep"), None),
            P(("grp", "ep"), None),
            P(("grp", "ep"), None, None),
            P(("grp", "ep")),
            P("grp"),
            P("grp", None),
            P(),
            P("grp", None, None),
            P("grp", None),
        ),
        out_specs=P(("grp", "ep"), None),
        check_vma=False,
    )
```

```python
import math

import jax
import jax.numpy as jnp
from jax import lax
from jax.sharding import PartitionSpec as P

TREE = 48
REQ_GRP = 4


def from_partner(block, axis, bit):
    count = lax.axis_size(axis)
    route = []
    for low in range(count):
        high = low | 1 << bit
        if high != low and high < count:
            route += [(low, high), (high, low)]
    return lax.ppermute(block, axis, route)


def bit_reversed(count):
    width = count.bit_length() - 1
    return [int(format(index, f"0{width}b")[::-1], 2) if width else 0 for index in range(count)]


def ancestors(parent_row):
    count = parent_row.shape[0]
    order = jnp.arange(count, dtype=jnp.int32)
    links = ((order[None, :] == parent_row[:, None]) & (order[:, None] > 0)).astype(jnp.float32)
    reach = jnp.eye(count, dtype=jnp.float32) + links
    for repeat in range(int(count).bit_length()):
        reach = jnp.minimum(jnp.dot(reach, reach, precision=lax.Precision.HIGHEST), 1.0)
    return reach > 0.5


def absorb(nope_rows, w_key):
    return jnp.einsum("thn,hrn->thr", nope_rows, w_key, preferred_element_type=jnp.float32).astype(
        jnp.bfloat16
    )


def append_partner(mine, partner, position, bit_level):
    upper_side = jnp.right_shift(position, bit_level) & 1 == 1
    former = jnp.where(upper_side, partner, mine)
    latter = jnp.where(upper_side, mine, partner)
    return jnp.concatenate([former, latter], axis=0)


def split_high(high):
    high_hi = high.astype(jnp.bfloat16)
    high_lo = (high - high_hi.astype(jnp.float32)).astype(jnp.bfloat16)
    return high_hi, high_lo


def pack_part(part_sum, part_high, part_total, width):
    high_hi, high_lo = split_high(part_high)
    stats = jnp.concatenate([high_hi, high_lo, part_total.astype(jnp.bfloat16)], axis=1)
    stats = jnp.pad(stats, ((0, 0), (0, width - stats.shape[1])))
    return jnp.concatenate([part_sum.astype(jnp.bfloat16), stats[:, None, :]], axis=1)


def unpack_part(packed, heads):
    stats = packed[:, heads].astype(jnp.float32)
    high = stats[:, :heads] + stats[:, heads : 2 * heads]
    total = stats[:, 2 * heads : 3 * heads]
    return packed[:, :heads].astype(jnp.float32), high, total


def combine_parts(kept_part, received):
    kept_sum, kept_high, kept_total = kept_part
    got_sum, got_high, got_total = received
    joint_high = jnp.maximum(kept_high, got_high)
    factor_kept = jnp.exp(kept_high - joint_high)
    factor_got = jnp.exp(got_high - joint_high)
    merged_sum = kept_sum * factor_kept[..., None] + got_sum * factor_got[..., None]
    merged_total = kept_total * factor_kept + got_total * factor_got
    return (merged_sum, joint_high, merged_total)


def per_device(
    q_nope,
    q_rope,
    tree_latent,
    cache_pool,
    page_table,
    cache_len,
    parents,
    w_key,
    w_value,
    out_weight,
):
    head_count = w_key.shape[0]
    latent_width = w_key.shape[1]
    nope_width = w_key.shape[2]
    token_count = q_nope.shape[0]
    rope_width = q_rope.shape[1] // head_count
    per_request = lax.axis_size("ep") // REQ_GRP
    grp_size = lax.axis_size("grp")
    doublings = per_request.bit_length() - 1
    position = lax.axis_index("ep")
    local_rank = position % per_request
    local_request = position // per_request
    score_scale = 1.0 / math.sqrt(nope_width + rope_width)
    raw_rows = jnp.concatenate([q_nope, q_rope], axis=1)
    for bit_level in reversed(range(doublings)):
        partner = from_partner(raw_rows, "ep", bit_level)
        raw_rows = append_partner(raw_rows, partner, position, bit_level)
    nope_rows = raw_rows[:, : q_nope.shape[1]].reshape(TREE, head_count, nope_width)
    rope_rows = raw_rows[:, q_nope.shape[1] :].reshape(TREE, head_count, rope_width)
    queries = jnp.concatenate([absorb(nope_rows, w_key), rope_rows], axis=2)
    cached = cache_pool.reshape(-1, cache_pool.shape[2])
    page_count, page_rows = cache_pool.shape[0], cache_pool.shape[1]
    pos_count = cached.shape[0]
    all_keys = jnp.concatenate([cached, tree_latent], axis=0)
    slots = jnp.arange(page_count, dtype=jnp.int32)
    logical_of_slot = jnp.sum(
        jnp.where(page_table[:, None] == slots[None, :], slots[:, None], 0), axis=0
    )
    place = (
        local_rank * pos_count
        + jnp.repeat(logical_of_slot, page_rows) * page_rows
        + jnp.tile(jnp.arange(page_rows, dtype=jnp.int32), page_count)
    )
    my_length = lax.dynamic_index_in_dim(cache_len, local_request, 0, keepdims=False)
    cache_ok = place < my_length
    parent_row = lax.dynamic_index_in_dim(parents, local_request, 0, keepdims=False)
    family = ancestors(parent_row)
    tree_cols = lax.dynamic_slice_in_dim(family, local_rank * token_count, token_count, 1)
    tree_ok = tree_cols.reshape(per_request, token_count, token_count)[
        jnp.array(bit_reversed(per_request))
    ].reshape(TREE, token_count)
    allowed = jnp.concatenate(
        [jnp.broadcast_to(cache_ok[None, :], (TREE, pos_count)), tree_ok], axis=1
    )
    scores = (
        jnp.einsum("ihl,kl->ihk", queries, all_keys, preferred_element_type=jnp.float32)
        * score_scale
    )
    masked = jnp.where(allowed[:, None, :], scores, -1e30)
    highest = jnp.max(masked, axis=2)
    powers = jnp.where(allowed[:, None, :], jnp.exp(masked - highest[..., None]), 0.0)
    total = jnp.sum(powers, axis=2)
    partial_value = jnp.einsum(
        "ihk,kr->ihr",
        powers.astype(jnp.bfloat16),
        all_keys[:, :latent_width],
        preferred_element_type=jnp.float32,
    )
    state = (partial_value, highest, total)
    for bit_level in range(doublings):
        half_rows = state[0].shape[0] // 2
        upper_side = jnp.right_shift(position, bit_level) & 1 == 1
        lower_part = tuple((member[:half_rows] for member in state))
        upper_part = tuple((member[half_rows:] for member in state))
        kept_part = tuple(
            (jnp.where(upper_side, upper, lower) for lower, upper in zip(lower_part, upper_part))
        )
        sent_part = tuple(
            (jnp.where(upper_side, lower, upper) for lower, upper in zip(lower_part, upper_part))
        )
        received = from_partner(pack_part(*sent_part, latent_width), "ep", bit_level)
        state = combine_parts(kept_part, unpack_part(received, head_count))
    merged_sum, merged_high, merged_total = state
    merged = merged_sum / merged_total[..., None]
    spread = lax.all_to_all(
        jnp.swapaxes(merged.astype(jnp.bfloat16), 0, 1), "grp", split_axis=0, concat_axis=0, tiled=True
    )
    spread = spread.reshape(grp_size, token_count, latent_width)[jnp.array(bit_reversed(grp_size))]
    head_rows = jnp.dot(
        spread.reshape(grp_size * token_count, latent_width),
        w_value[0],
        preferred_element_type=jnp.float32,
    ).astype(jnp.bfloat16)
    rows_out = jnp.dot(head_rows, out_weight, preferred_element_type=jnp.float32)
    group = lax.axis_index("grp")
    for bit_level in range(grp_size.bit_length() - 1):
        half_rows = rows_out.shape[0] // 2
        upper_side = jnp.right_shift(group, bit_level) & 1 == 1
        lower, upper = rows_out[:half_rows], rows_out[half_rows:]
        kept = jnp.where(upper_side, upper, lower)
        sent = jnp.where(upper_side, lower, upper)
        rows_out = kept + from_partner(sent.astype(jnp.bfloat16), "grp", bit_level).astype(
            jnp.float32
        )
    return rows_out.astype(jnp.bfloat16)


def solution(mesh):
    return jax.shard_map(
        per_device,
        mesh=mesh,
        in_specs=(
            P(("grp", "ep"), None),
            P(("grp", "ep"), None),
            P(("grp", "ep"), None),
            P(("grp", "ep"), None, None),
            P(("grp", "ep")),
            P("grp"),
            P("grp", None),
            P(),
            P("grp", None, None),
            P("grp", None),
        ),
        out_specs=P(("grp", "ep"), None),
        check_vma=False,
    )
```

```python
import math

import jax
import jax.numpy as jnp
from jax import lax
from jax.sharding import PartitionSpec as P

TREE = 48
REQ_GRP = 4


def from_partner(block, axis, bit):
    count = lax.axis_size(axis)
    route = []
    for low in range(count):
        high = low | 1 << bit
        if high != low and high < count:
            route += [(low, high), (high, low)]
    return lax.ppermute(block, axis, route)


def shifted(block, axis, group, shift):
    count = lax.axis_size(axis)
    route = [(i, (i // group) * group + (i % group + shift) % group) for i in range(count)]
    return lax.ppermute(block, axis, route)


def bit_reversed(count):
    width = count.bit_length() - 1
    return [int(format(index, f"0{width}b")[::-1], 2) if width else 0 for index in range(count)]


def ancestors(parent_row):
    count = parent_row.shape[0]
    order = jnp.arange(count, dtype=jnp.int32)
    links = ((order[None, :] == parent_row[:, None]) & (order[:, None] > 0)).astype(jnp.float32)
    reach = jnp.eye(count, dtype=jnp.float32) + links
    for repeat in range(int(count).bit_length()):
        reach = jnp.minimum(jnp.dot(reach, reach, precision=lax.Precision.HIGHEST), 1.0)
    return reach > 0.5


def absorb(nope_rows, w_key):
    return jnp.einsum("thn,hrn->thr", nope_rows, w_key, preferred_element_type=jnp.float32).astype(
        jnp.bfloat16
    )


def append_partner(mine, partner, position, bit_level):
    upper_side = jnp.right_shift(position, bit_level) & 1 == 1
    former = jnp.where(upper_side, partner, mine)
    latter = jnp.where(upper_side, mine, partner)
    return jnp.concatenate([former, latter], axis=0)


def split_high(high):
    high_hi = high.astype(jnp.bfloat16)
    high_lo = (high - high_hi.astype(jnp.float32)).astype(jnp.bfloat16)
    return high_hi, high_lo


def pack_part(part_sum, part_high, part_total, width):
    high_hi, high_lo = split_high(part_high)
    stats = jnp.concatenate([high_hi, high_lo, part_total.astype(jnp.bfloat16)], axis=1)
    stats = jnp.pad(stats, ((0, 0), (0, width - stats.shape[1])))
    return jnp.concatenate([part_sum.astype(jnp.bfloat16), stats[:, None, :]], axis=1)


def unpack_part(packed, heads):
    stats = packed[:, heads].astype(jnp.float32)
    high = stats[:, :heads] + stats[:, heads : 2 * heads]
    total = stats[:, 2 * heads : 3 * heads]
    return packed[:, :heads].astype(jnp.float32), high, total


def combine_parts(kept_part, received):
    kept_sum, kept_high, kept_total = kept_part
    got_sum, got_high, got_total = received
    joint_high = jnp.maximum(kept_high, got_high)
    factor_kept = jnp.exp(kept_high - joint_high)
    factor_got = jnp.exp(got_high - joint_high)
    merged_sum = kept_sum * factor_kept[..., None] + got_sum * factor_got[..., None]
    merged_total = kept_total * factor_kept + got_total * factor_got
    return (merged_sum, joint_high, merged_total)


def per_device(
    q_nope,
    q_rope,
    tree_latent,
    cache_pool,
    page_table,
    cache_len,
    parents,
    w_key,
    w_value,
    out_weight,
):
    head_count = w_key.shape[0]
    latent_width = w_key.shape[1]
    nope_width = w_key.shape[2]
    token_count = q_nope.shape[0]
    rope_width = q_rope.shape[1] // head_count
    per_request = lax.axis_size("ep") // REQ_GRP
    grp_size = lax.axis_size("grp")
    doublings = per_request.bit_length() - 1
    position = lax.axis_index("ep")
    local_rank = position % per_request
    local_request = position // per_request
    score_scale = 1.0 / math.sqrt(nope_width + rope_width)
    raw_rows = jnp.concatenate([q_nope, q_rope], axis=1)
    for bit_level in reversed(range(doublings)):
        partner = from_partner(raw_rows, "ep", bit_level)
        raw_rows = append_partner(raw_rows, partner, position, bit_level)
    nope_rows = raw_rows[:, : q_nope.shape[1]].reshape(TREE, head_count, nope_width)
    rope_rows = raw_rows[:, q_nope.shape[1] :].reshape(TREE, head_count, rope_width)
    queries = jnp.concatenate([absorb(nope_rows, w_key), rope_rows], axis=2)
    cached = cache_pool.reshape(-1, cache_pool.shape[2])
    page_count, page_rows = cache_pool.shape[0], cache_pool.shape[1]
    pos_count = cached.shape[0]
    all_keys = jnp.concatenate([cached, tree_latent], axis=0)
    slots = jnp.arange(page_count, dtype=jnp.int32)
    logical_of_slot = jnp.sum(
        jnp.where(page_table[:, None] == slots[None, :], slots[:, None], 0), axis=0
    )
    place = (
        local_rank * pos_count
        + jnp.repeat(logical_of_slot, page_rows) * page_rows
        + jnp.tile(jnp.arange(page_rows, dtype=jnp.int32), page_count)
    )
    my_length = lax.dynamic_index_in_dim(cache_len, local_request, 0, keepdims=False)
    cache_ok = place < my_length
    parent_row = lax.dynamic_index_in_dim(parents, local_request, 0, keepdims=False)
    family = ancestors(parent_row)
    tree_cols = lax.dynamic_slice_in_dim(family, local_rank * token_count, token_count, 1)
    tree_ok = tree_cols.reshape(per_request, token_count, token_count)[
        jnp.array(bit_reversed(per_request))
    ].reshape(TREE, token_count)
    allowed = jnp.concatenate(
        [jnp.broadcast_to(cache_ok[None, :], (TREE, pos_count)), tree_ok], axis=1
    )
    scores = (
        jnp.einsum("ihl,kl->ihk", queries, all_keys, preferred_element_type=jnp.float32)
        * score_scale
    )
    masked = jnp.where(allowed[:, None, :], scores, -1e30)
    highest = jnp.max(masked, axis=2)
    powers = jnp.where(allowed[:, None, :], jnp.exp(masked - highest[..., None]), 0.0)
    total = jnp.sum(powers, axis=2)
    partial_value = jnp.einsum(
        "ihk,kr->ihr",
        powers.astype(jnp.bfloat16),
        all_keys[:, :latent_width],
        preferred_element_type=jnp.float32,
    )
    state = (partial_value, highest, total)
    for bit_level in range(doublings):
        half_rows = state[0].shape[0] // 2
        upper_side = jnp.right_shift(position, bit_level) & 1 == 1
        lower_part = tuple((member[:half_rows] for member in state))
        upper_part = tuple((member[half_rows:] for member in state))
        kept_part = tuple(
            (jnp.where(upper_side, upper, lower) for lower, upper in zip(lower_part, upper_part))
        )
        sent_part = tuple(
            (jnp.where(upper_side, lower, upper) for lower, upper in zip(lower_part, upper_part))
        )
        received = from_partner(pack_part(*sent_part, latent_width), "ep", bit_level)
        state = combine_parts(kept_part, unpack_part(received, head_count))
    merged_sum, merged_high, merged_total = state
    merged = merged_sum / merged_total[..., None]
    spread = lax.all_to_all(
        jnp.swapaxes(merged.astype(jnp.bfloat16), 0, 1), "grp", split_axis=0, concat_axis=0, tiled=True
    )
    spread = spread.reshape(grp_size, token_count, latent_width)[jnp.array(bit_reversed(grp_size))]
    head_rows = jnp.dot(
        spread.reshape(grp_size * token_count, latent_width),
        w_value[0],
        preferred_element_type=jnp.float32,
    ).astype(jnp.bfloat16)
    rows_out = jnp.dot(head_rows, out_weight, preferred_element_type=jnp.float32)
    group = lax.axis_index("grp")
    for bit_level in range(2):
        half_rows = rows_out.shape[0] // 2
        upper_side = jnp.right_shift(group, bit_level) & 1 == 1
        lower, upper = rows_out[:half_rows], rows_out[half_rows:]
        kept = jnp.where(upper_side, upper, lower)
        sent = jnp.where(upper_side, lower, upper)
        rows_out = kept + from_partner(sent.astype(jnp.bfloat16), "grp", bit_level).astype(
            jnp.float32
        )
    ring = grp_size // 4
    blocks = rows_out.reshape(ring, token_count, rows_out.shape[1])
    mine = group // 4

    def block_for(member):
        return lax.dynamic_index_in_dim(
            blocks, (member & 1) * 2 + member // 2, 0, keepdims=False
        )

    total_rows = block_for(mine)
    for step in range(1, ring):
        sent = block_for((mine + step) % ring).astype(jnp.bfloat16)
        total_rows = total_rows + shifted(sent, "grp", grp_size, 4 * step).astype(jnp.float32)
    return total_rows.astype(jnp.bfloat16)


def solution(mesh):
    return jax.shard_map(
        per_device,
        mesh=mesh,
        in_specs=(
            P(("grp", "ep"), None),
            P(("grp", "ep"), None),
            P(("grp", "ep"), None),
            P(("grp", "ep"), None, None),
            P(("grp", "ep")),
            P("grp"),
            P("grp", None),
            P(),
            P("grp", None, None),
            P("grp", None),
        ),
        out_specs=P(("grp", "ep"), None),
        check_vma=False,
    )
```

```python
import math

import jax
import jax.numpy as jnp
from jax import lax
from jax.sharding import PartitionSpec as P

TREE = 48
REQ_GRP = 4


def from_partner(block, axis, bit):
    count = lax.axis_size(axis)
    route = []
    for low in range(count):
        high = low | 1 << bit
        if high != low and high < count:
            route += [(low, high), (high, low)]
    return lax.ppermute(block, axis, route)


def shifted(block, axis, group, shift):
    count = lax.axis_size(axis)
    route = [(i, (i // group) * group + (i % group + shift) % group) for i in range(count)]
    return lax.ppermute(block, axis, route)


def bit_reversed(count):
    width = count.bit_length() - 1
    return [int(format(index, f"0{width}b")[::-1], 2) if width else 0 for index in range(count)]


def ancestors(parent_row):
    count = parent_row.shape[0]
    order = jnp.arange(count, dtype=jnp.int32)
    links = ((order[None, :] == parent_row[:, None]) & (order[:, None] > 0)).astype(jnp.float32)
    reach = jnp.eye(count, dtype=jnp.float32) + links
    for repeat in range(int(count).bit_length()):
        reach = jnp.minimum(jnp.dot(reach, reach, precision=lax.Precision.HIGHEST), 1.0)
    return reach > 0.5


def absorb(nope_rows, w_key):
    return jnp.einsum("thn,hrn->thr", nope_rows, w_key, preferred_element_type=jnp.float32).astype(
        jnp.bfloat16
    )


def append_partner(mine, partner, position, bit_level):
    upper_side = jnp.right_shift(position, bit_level) & 1 == 1
    former = jnp.where(upper_side, partner, mine)
    latter = jnp.where(upper_side, mine, partner)
    return jnp.concatenate([former, latter], axis=0)


def split_high(high):
    high_hi = high.astype(jnp.bfloat16)
    high_lo = (high - high_hi.astype(jnp.float32)).astype(jnp.bfloat16)
    return high_hi, high_lo


def pack_part(part_sum, part_high, part_total, width):
    high_hi, high_lo = split_high(part_high)
    stats = jnp.concatenate([high_hi, high_lo, part_total.astype(jnp.bfloat16)], axis=1)
    stats = jnp.pad(stats, ((0, 0), (0, width - stats.shape[1])))
    rows, heads = part_sum.shape[0], part_sum.shape[1]
    flat_sum = part_sum.astype(jnp.bfloat16).reshape(rows * heads, width)
    return jnp.concatenate([flat_sum, stats], axis=0)


def unpack_part(packed, heads):
    rows = packed.shape[0] // (heads + 1)
    stats = packed[rows * heads :].astype(jnp.float32)
    high = stats[:, :heads] + stats[:, heads : 2 * heads]
    total = stats[:, 2 * heads : 3 * heads]
    part_sum = packed[: rows * heads].reshape(rows, heads, packed.shape[1])
    return part_sum.astype(jnp.float32), high, total


def combine_parts(kept_part, received):
    kept_sum, kept_high, kept_total = kept_part
    got_sum, got_high, got_total = received
    joint_high = jnp.maximum(kept_high, got_high)
    factor_kept = jnp.exp(kept_high - joint_high)
    factor_got = jnp.exp(got_high - joint_high)
    merged_sum = kept_sum * factor_kept[..., None] + got_sum * factor_got[..., None]
    merged_total = kept_total * factor_kept + got_total * factor_got
    return (merged_sum, joint_high, merged_total)


def per_device(
    q_nope,
    q_rope,
    tree_latent,
    cache_pool,
    page_table,
    cache_len,
    parents,
    w_key,
    w_value,
    out_weight,
):
    head_count = w_key.shape[0]
    latent_width = w_key.shape[1]
    nope_width = w_key.shape[2]
    token_count = q_nope.shape[0]
    rope_width = q_rope.shape[1] // head_count
    per_request = lax.axis_size("ep") // REQ_GRP
    grp_size = lax.axis_size("grp")
    doublings = per_request.bit_length() - 1
    position = lax.axis_index("ep")
    local_rank = position % per_request
    local_request = position // per_request
    score_scale = 1.0 / math.sqrt(nope_width + rope_width)
    raw_rows = jnp.concatenate([q_nope, q_rope], axis=1)
    for bit_level in reversed(range(doublings)):
        partner = from_partner(raw_rows, "ep", bit_level)
        raw_rows = append_partner(raw_rows, partner, position, bit_level)
    nope_rows = raw_rows[:, : q_nope.shape[1]].reshape(TREE, head_count, nope_width)
    rope_rows = raw_rows[:, q_nope.shape[1] :].reshape(TREE, head_count, rope_width)
    queries = jnp.concatenate([absorb(nope_rows, w_key), rope_rows], axis=2)
    cached = cache_pool.reshape(-1, cache_pool.shape[2])
    page_count, page_rows = cache_pool.shape[0], cache_pool.shape[1]
    pos_count = cached.shape[0]
    all_keys = jnp.concatenate([cached, tree_latent], axis=0)
    slots = jnp.arange(page_count, dtype=jnp.int32)
    logical_of_slot = jnp.sum(
        jnp.where(page_table[:, None] == slots[None, :], slots[:, None], 0), axis=0
    )
    place = (
        local_rank * pos_count
        + jnp.repeat(logical_of_slot, page_rows) * page_rows
        + jnp.tile(jnp.arange(page_rows, dtype=jnp.int32), page_count)
    )
    my_length = lax.dynamic_index_in_dim(cache_len, local_request, 0, keepdims=False)
    cache_ok = place < my_length
    parent_row = lax.dynamic_index_in_dim(parents, local_request, 0, keepdims=False)
    family = ancestors(parent_row)
    tree_cols = lax.dynamic_slice_in_dim(family, local_rank * token_count, token_count, 1)
    tree_ok = tree_cols.reshape(per_request, token_count, token_count)[
        jnp.array(bit_reversed(per_request))
    ].reshape(TREE, token_count)
    allowed = jnp.concatenate(
        [jnp.broadcast_to(cache_ok[None, :], (TREE, pos_count)), tree_ok], axis=1
    )
    scores = (
        jnp.einsum("ihl,kl->ihk", queries, all_keys, preferred_element_type=jnp.float32)
        * score_scale
    )
    masked = jnp.where(allowed[:, None, :], scores, -1e30)
    highest = jnp.max(masked, axis=2)
    powers = jnp.where(allowed[:, None, :], jnp.exp(masked - highest[..., None]), 0.0)
    total = jnp.sum(powers, axis=2)
    partial_value = jnp.einsum(
        "ihk,kr->ihr",
        powers.astype(jnp.bfloat16),
        all_keys[:, :latent_width],
        preferred_element_type=jnp.float32,
    )
    state = (partial_value, highest, total)
    for bit_level in range(doublings):
        half_rows = state[0].shape[0] // 2
        upper_side = jnp.right_shift(position, bit_level) & 1 == 1
        lower_part = tuple((member[:half_rows] for member in state))
        upper_part = tuple((member[half_rows:] for member in state))
        kept_part = tuple(
            (jnp.where(upper_side, upper, lower) for lower, upper in zip(lower_part, upper_part))
        )
        sent_part = tuple(
            (jnp.where(upper_side, lower, upper) for lower, upper in zip(lower_part, upper_part))
        )
        received = from_partner(pack_part(*sent_part, latent_width), "ep", bit_level)
        state = combine_parts(kept_part, unpack_part(received, head_count))
    merged_sum, merged_high, merged_total = state
    merged = merged_sum / merged_total[..., None]
    spread = lax.all_to_all(
        jnp.swapaxes(merged.astype(jnp.bfloat16), 0, 1), "grp", split_axis=0, concat_axis=0, tiled=True
    )
    spread = spread.reshape(grp_size, token_count, latent_width)[jnp.array(bit_reversed(grp_size))]
    head_rows = jnp.dot(
        spread.reshape(grp_size * token_count, latent_width),
        w_value[0],
        preferred_element_type=jnp.float32,
    ).astype(jnp.bfloat16)
    rows_out = jnp.dot(head_rows, out_weight, preferred_element_type=jnp.float32)
    group = lax.axis_index("grp")
    for bit_level in range(2):
        half_rows = rows_out.shape[0] // 2
        upper_side = jnp.right_shift(group, bit_level) & 1 == 1
        lower, upper = rows_out[:half_rows], rows_out[half_rows:]
        kept = jnp.where(upper_side, upper, lower)
        sent = jnp.where(upper_side, lower, upper)
        rows_out = kept + from_partner(sent.astype(jnp.bfloat16), "grp", bit_level).astype(
            jnp.float32
        )
    ring = grp_size // 4
    blocks = rows_out.reshape(ring, token_count, rows_out.shape[1])
    mine = group // 4

    def block_for(member):
        return lax.dynamic_index_in_dim(
            blocks, (member & 1) * 2 + member // 2, 0, keepdims=False
        )

    total_rows = block_for(mine)
    for step in range(1, ring):
        sent = block_for((mine + step) % ring).astype(jnp.bfloat16)
        total_rows = total_rows + shifted(sent, "grp", grp_size, 4 * step).astype(jnp.float32)
    return total_rows.astype(jnp.bfloat16)


def solution(mesh):
    return jax.shard_map(
        per_device,
        mesh=mesh,
        in_specs=(
            P(("grp", "ep"), None),
            P(("grp", "ep"), None),
            P(("grp", "ep"), None),
            P(("grp", "ep"), None, None),
            P(("grp", "ep")),
            P("grp"),
            P("grp", None),
            P(),
            P("grp", None, None),
            P("grp", None),
        ),
        out_specs=P(("grp", "ep"), None),
        check_vma=False,
    )
```

```python
import math

import jax
import jax.numpy as jnp
from jax import lax
from jax.sharding import PartitionSpec as P

TREE = 48
REQ_GRP = 4


def from_partner(block, axis, bit):
    count = lax.axis_size(axis)
    route = []
    for low in range(count):
        high = low | 1 << bit
        if high != low and high < count:
            route += [(low, high), (high, low)]
    return lax.ppermute(block, axis, route)


def shifted(block, axis, group, shift):
    count = lax.axis_size(axis)
    route = [(i, (i // group) * group + (i % group + shift) % group) for i in range(count)]
    return lax.ppermute(block, axis, route)


def bit_reversed(count):
    width = count.bit_length() - 1
    return [int(format(index, f"0{width}b")[::-1], 2) if width else 0 for index in range(count)]


def ancestors(parent_row):
    count = parent_row.shape[0]
    order = jnp.arange(count, dtype=jnp.int32)
    links = ((order[None, :] == parent_row[:, None]) & (order[:, None] > 0)).astype(jnp.float32)
    reach = jnp.eye(count, dtype=jnp.float32) + links
    for repeat in range(int(count).bit_length()):
        reach = jnp.minimum(jnp.dot(reach, reach, precision=lax.Precision.HIGHEST), 1.0)
    return reach > 0.5


def absorb(nope_rows, w_key):
    return jnp.einsum("thn,hrn->thr", nope_rows, w_key, preferred_element_type=jnp.float32).astype(
        jnp.bfloat16
    )


def append_partner(mine, partner, position, bit_level):
    upper_side = jnp.right_shift(position, bit_level) & 1 == 1
    former = jnp.where(upper_side, partner, mine)
    latter = jnp.where(upper_side, mine, partner)
    return jnp.concatenate([former, latter], axis=0)


def split_high(high):
    high_hi = high.astype(jnp.bfloat16)
    high_lo = (high - high_hi.astype(jnp.float32)).astype(jnp.bfloat16)
    return high_hi, high_lo


def pack_part(part_sum, part_high, part_total, width):
    high_hi, high_lo = split_high(part_high)
    stats = jnp.concatenate([high_hi, high_lo, part_total.astype(jnp.bfloat16)], axis=1)
    stats = jnp.pad(stats, ((0, 0), (0, width - stats.shape[1])))
    rows, heads = part_sum.shape[0], part_sum.shape[1]
    flat_sum = part_sum.astype(jnp.bfloat16).reshape(rows * heads, width)
    return jnp.concatenate([flat_sum, stats], axis=0)


def unpack_part(packed, heads):
    rows = packed.shape[0] // (heads + 1)
    stats = packed[rows * heads :].astype(jnp.float32)
    high = stats[:, :heads] + stats[:, heads : 2 * heads]
    total = stats[:, 2 * heads : 3 * heads]
    part_sum = packed[: rows * heads].reshape(rows, heads, packed.shape[1])
    return part_sum.astype(jnp.float32), high, total


def combine_parts(kept_part, received):
    kept_sum, kept_high, kept_total = kept_part
    got_sum, got_high, got_total = received
    joint_high = jnp.maximum(kept_high, got_high)
    factor_kept = jnp.exp(kept_high - joint_high)
    factor_got = jnp.exp(got_high - joint_high)
    merged_sum = kept_sum * factor_kept[..., None] + got_sum * factor_got[..., None]
    merged_total = kept_total * factor_kept + got_total * factor_got
    return (merged_sum, joint_high, merged_total)


def per_device(
    q_nope,
    q_rope,
    tree_latent,
    cache_pool,
    page_table,
    cache_len,
    parents,
    w_key,
    w_value,
    out_weight,
):
    head_count = w_key.shape[0]
    latent_width = w_key.shape[1]
    nope_width = w_key.shape[2]
    token_count = q_nope.shape[0]
    rope_width = q_rope.shape[1] // head_count
    per_request = lax.axis_size("ep") // REQ_GRP
    grp_size = lax.axis_size("grp")
    doublings = per_request.bit_length() - 1
    position = lax.axis_index("ep")
    local_rank = position % per_request
    local_request = position // per_request
    score_scale = 1.0 / math.sqrt(nope_width + rope_width)
    raw_rows = jnp.concatenate([q_nope, q_rope], axis=1)
    for bit_level in reversed(range(doublings)):
        partner = from_partner(raw_rows, "ep", bit_level)
        raw_rows = append_partner(raw_rows, partner, position, bit_level)
    nope_rows = raw_rows[:, : q_nope.shape[1]].reshape(TREE, head_count, nope_width)
    rope_rows = raw_rows[:, q_nope.shape[1] :].reshape(TREE, head_count, rope_width)
    queries = jnp.concatenate([absorb(nope_rows, w_key), rope_rows], axis=2)
    cached = cache_pool.reshape(-1, cache_pool.shape[2])
    page_count, page_rows = cache_pool.shape[0], cache_pool.shape[1]
    pos_count = cached.shape[0]
    all_keys = jnp.concatenate([cached, tree_latent], axis=0)
    slots = jnp.arange(page_count, dtype=jnp.int32)
    logical_of_slot = jnp.sum(
        jnp.where(page_table[:, None] == slots[None, :], slots[:, None], 0), axis=0
    )
    place = (
        local_rank * pos_count
        + jnp.repeat(logical_of_slot, page_rows) * page_rows
        + jnp.tile(jnp.arange(page_rows, dtype=jnp.int32), page_count)
    )
    my_length = lax.dynamic_index_in_dim(cache_len, local_request, 0, keepdims=False)
    cache_ok = place < my_length
    parent_row = lax.dynamic_index_in_dim(parents, local_request, 0, keepdims=False)
    family = ancestors(parent_row)
    tree_cols = lax.dynamic_slice_in_dim(family, local_rank * token_count, token_count, 1)
    tree_ok = tree_cols.reshape(per_request, token_count, token_count)[
        jnp.array(bit_reversed(per_request))
    ].reshape(TREE, token_count)
    allowed = jnp.concatenate(
        [jnp.broadcast_to(cache_ok[None, :], (TREE, pos_count)), tree_ok], axis=1
    )
    scores = (
        jnp.einsum("ihl,kl->ihk", queries, all_keys, preferred_element_type=jnp.float32)
        * score_scale
    )
    masked = jnp.where(allowed[:, None, :], scores, -1e30)
    highest = jnp.max(masked, axis=2)
    powers = jnp.where(allowed[:, None, :], jnp.exp(masked - highest[..., None]), 0.0)
    total = jnp.sum(powers, axis=2)
    partial_value = jnp.einsum(
        "ihk,kr->ihr",
        powers.astype(jnp.bfloat16),
        all_keys[:, :latent_width],
        preferred_element_type=jnp.float32,
    )
    state = (partial_value, highest, total)
    for bit_level in range(doublings):
        half_rows = state[0].shape[0] // 2
        upper_side = jnp.right_shift(position, bit_level) & 1 == 1
        lower_part = tuple((member[:half_rows] for member in state))
        upper_part = tuple((member[half_rows:] for member in state))
        kept_part = tuple(
            (jnp.where(upper_side, upper, lower) for lower, upper in zip(lower_part, upper_part))
        )
        sent_part = tuple(
            (jnp.where(upper_side, lower, upper) for lower, upper in zip(lower_part, upper_part))
        )
        received = from_partner(pack_part(*sent_part, latent_width), "ep", bit_level)
        state = combine_parts(kept_part, unpack_part(received, head_count))
    merged_sum, merged_high, merged_total = state
    merged = merged_sum / merged_total[..., None]
    spread = lax.all_to_all(
        jnp.swapaxes(merged.astype(jnp.bfloat16), 0, 1), "grp", split_axis=0, concat_axis=0, tiled=True
    )
    group = lax.axis_index("grp")
    core = position & 1
    label = (group - core) % grp_size
    spread = jnp.take(
        spread.reshape(grp_size, token_count, latent_width),
        (jnp.array(bit_reversed(grp_size)) + core) % grp_size,
        axis=0,
    )
    head_rows = jnp.dot(
        spread.reshape(grp_size * token_count, latent_width),
        w_value[0],
        preferred_element_type=jnp.float32,
    ).astype(jnp.bfloat16)
    rows_out = jnp.dot(head_rows, out_weight, preferred_element_type=jnp.float32)
    ep_size = lax.axis_size("ep")
    for bit_level in range(2):
        half_rows = rows_out.shape[0] // 2
        upper_side = jnp.right_shift(label, bit_level) & 1 == 1
        lower, upper = rows_out[:half_rows], rows_out[half_rows:]
        kept = jnp.where(upper_side, upper, lower)
        sent = jnp.where(upper_side, lower, upper)
        route = []
        for plane in range(grp_size):
            for column in range(ep_size):
                shift = column & 1
                other = ((((plane - shift) % grp_size) ^ (1 << bit_level)) + shift) % grp_size
                route.append((plane * ep_size + column, other * ep_size + column))
        got = lax.ppermute(sent.astype(jnp.bfloat16), ("grp", "ep"), route)
        rows_out = kept + got.astype(jnp.float32)
    ring = grp_size // 4
    blocks = rows_out.reshape(ring, token_count, rows_out.shape[1])
    mine = label // 4

    def block_for(member):
        return lax.dynamic_index_in_dim(
            blocks, (member & 1) * 2 + member // 2, 0, keepdims=False
        )

    total_rows = block_for(mine)
    for step in range(1, ring):
        sent = block_for((mine + step) % ring).astype(jnp.bfloat16)
        total_rows = total_rows + shifted(sent, "grp", grp_size, 4 * step).astype(jnp.float32)
    return total_rows.astype(jnp.bfloat16)


def solution(mesh):
    return jax.shard_map(
        per_device,
        mesh=mesh,
        in_specs=(
            P(("grp", "ep"), None),
            P(("grp", "ep"), None),
            P(("grp", "ep"), None),
            P(("grp", "ep"), None, None),
            P(("grp", "ep")),
            P("grp"),
            P("grp", None),
            P(),
            P("grp", None, None),
            P("grp", None),
        ),
        out_specs=P(("grp", "ep"), None),
        check_vma=False,
    )
```

```python
import math

import jax
import jax.numpy as jnp
from jax import lax
from jax.sharding import PartitionSpec as P

TREE = 48
REQ_GRP = 4


def from_partner(block, axis, bit):
    count = lax.axis_size(axis)
    route = []
    for low in range(count):
        high = low | 1 << bit
        if high != low and high < count:
            route += [(low, high), (high, low)]
    return lax.ppermute(block, axis, route)


def shifted(block, axis, group, shift):
    count = lax.axis_size(axis)
    route = [(i, (i // group) * group + (i % group + shift) % group) for i in range(count)]
    return lax.ppermute(block, axis, route)


def bit_reversed(count):
    width = count.bit_length() - 1
    return [int(format(index, f"0{width}b")[::-1], 2) if width else 0 for index in range(count)]


def ancestors(parent_row):
    count = parent_row.shape[0]
    order = jnp.arange(count, dtype=jnp.int32)
    links = ((order[None, :] == parent_row[:, None]) & (order[:, None] > 0)).astype(jnp.float32)
    reach = jnp.eye(count, dtype=jnp.float32) + links
    for repeat in range(int(count).bit_length()):
        reach = jnp.minimum(jnp.dot(reach, reach, precision=lax.Precision.HIGHEST), 1.0)
    return reach > 0.5


def absorb(nope_rows, w_key):
    return jnp.einsum("thn,hrn->thr", nope_rows, w_key, preferred_element_type=jnp.float32).astype(
        jnp.bfloat16
    )


def append_partner(mine, partner, position, bit_level):
    upper_side = jnp.right_shift(position, bit_level) & 1 == 1
    former = jnp.where(upper_side, partner, mine)
    latter = jnp.where(upper_side, mine, partner)
    return jnp.concatenate([former, latter], axis=0)


def split_high(high):
    high_hi = high.astype(jnp.bfloat16)
    high_lo = (high - high_hi.astype(jnp.float32)).astype(jnp.bfloat16)
    return high_hi, high_lo


def pack_part(part_sum, part_high, part_total, width):
    high_hi, high_lo = split_high(part_high)
    stats = jnp.concatenate([high_hi, high_lo, part_total.astype(jnp.bfloat16)], axis=1)
    stats = jnp.pad(stats, ((0, 0), (0, width - stats.shape[1])))
    rows, heads = part_sum.shape[0], part_sum.shape[1]
    flat_sum = part_sum.astype(jnp.bfloat16).reshape(rows * heads, width)
    return jnp.concatenate([flat_sum, stats], axis=0)


def unpack_part(packed, heads):
    rows = packed.shape[0] // (heads + 1)
    stats = packed[rows * heads :].astype(jnp.float32)
    high = stats[:, :heads] + stats[:, heads : 2 * heads]
    total = stats[:, 2 * heads : 3 * heads]
    part_sum = packed[: rows * heads].reshape(rows, heads, packed.shape[1])
    return part_sum.astype(jnp.float32), high, total


def combine_parts(kept_part, received):
    kept_sum, kept_high, kept_total = kept_part
    got_sum, got_high, got_total = received
    joint_high = jnp.maximum(kept_high, got_high)
    factor_kept = jnp.exp(kept_high - joint_high)
    factor_got = jnp.exp(got_high - joint_high)
    merged_sum = kept_sum * factor_kept[..., None] + got_sum * factor_got[..., None]
    merged_total = kept_total * factor_kept + got_total * factor_got
    return (merged_sum, joint_high, merged_total)


def per_device(
    q_nope,
    q_rope,
    tree_latent,
    cache_pool,
    page_table,
    cache_len,
    parents,
    w_key,
    w_value,
    out_weight,
):
    head_count = w_key.shape[0]
    latent_width = w_key.shape[1]
    nope_width = w_key.shape[2]
    token_count = q_nope.shape[0]
    rope_width = q_rope.shape[1] // head_count
    per_request = lax.axis_size("ep") // REQ_GRP
    grp_size = lax.axis_size("grp")
    doublings = per_request.bit_length() - 1
    position = lax.axis_index("ep")
    local_rank = position % per_request
    local_request = position // per_request
    score_scale = 1.0 / math.sqrt(nope_width + rope_width)
    raw_rows = jnp.concatenate([q_nope, q_rope], axis=1)
    for bit_level in reversed(range(doublings)):
        partner = from_partner(raw_rows, "ep", bit_level)
        raw_rows = append_partner(raw_rows, partner, position, bit_level)
    nope_rows = raw_rows[:, : q_nope.shape[1]].reshape(TREE, head_count, nope_width)
    rope_rows = raw_rows[:, q_nope.shape[1] :].reshape(TREE, head_count, rope_width)
    queries = jnp.concatenate([absorb(nope_rows, w_key), rope_rows], axis=2)
    cached = cache_pool.reshape(-1, cache_pool.shape[2])
    page_count, page_rows = cache_pool.shape[0], cache_pool.shape[1]
    pos_count = cached.shape[0]
    all_keys = jnp.concatenate([cached, tree_latent], axis=0)
    slots = jnp.arange(page_count, dtype=jnp.int32)
    logical_of_slot = jnp.sum(
        jnp.where(page_table[:, None] == slots[None, :], slots[:, None], 0), axis=0
    )
    place = (
        local_rank * pos_count
        + jnp.repeat(logical_of_slot, page_rows) * page_rows
        + jnp.tile(jnp.arange(page_rows, dtype=jnp.int32), page_count)
    )
    my_length = lax.dynamic_index_in_dim(cache_len, local_request, 0, keepdims=False)
    cache_ok = place < my_length
    parent_row = lax.dynamic_index_in_dim(parents, local_request, 0, keepdims=False)
    family = ancestors(parent_row)
    tree_cols = lax.dynamic_slice_in_dim(family, local_rank * token_count, token_count, 1)
    tree_ok = tree_cols.reshape(per_request, token_count, token_count)[
        jnp.array(bit_reversed(per_request))
    ].reshape(TREE, token_count)
    allowed = jnp.concatenate(
        [jnp.broadcast_to(cache_ok[None, :], (TREE, pos_count)), tree_ok], axis=1
    )
    scores = (
        jnp.einsum("ihl,kl->ihk", queries, all_keys, preferred_element_type=jnp.float32)
        * score_scale
    )
    masked = jnp.where(allowed[:, None, :], scores, -1e30)
    highest = jnp.max(masked, axis=2)
    powers = jnp.where(allowed[:, None, :], jnp.exp(masked - highest[..., None]), 0.0)
    total = jnp.sum(powers, axis=2)
    partial_value = jnp.einsum(
        "ihk,kr->ihr",
        powers.astype(jnp.bfloat16),
        all_keys[:, :latent_width],
        preferred_element_type=jnp.float32,
    )
    state = (partial_value, highest, total)
    for bit_level in range(doublings):
        half_rows = state[0].shape[0] // 2
        upper_side = jnp.right_shift(position, bit_level) & 1 == 1
        lower_part = tuple((member[:half_rows] for member in state))
        upper_part = tuple((member[half_rows:] for member in state))
        kept_part = tuple(
            (jnp.where(upper_side, upper, lower) for lower, upper in zip(lower_part, upper_part))
        )
        sent_part = tuple(
            (jnp.where(upper_side, lower, upper) for lower, upper in zip(lower_part, upper_part))
        )
        received = from_partner(pack_part(*sent_part, latent_width), "ep", bit_level)
        state = combine_parts(kept_part, unpack_part(received, head_count))
    merged_sum, merged_high, merged_total = state
    merged = merged_sum / merged_total[..., None]
    chunk = jnp.swapaxes(merged.astype(jnp.bfloat16), 0, 1).reshape(grp_size, -1, 128)
    spread = lax.all_to_all(chunk, "grp", split_axis=0, concat_axis=0, tiled=True)
    spread = spread.reshape(grp_size, token_count, latent_width)[jnp.array(bit_reversed(grp_size))]
    head_rows = jnp.dot(
        spread.reshape(grp_size * token_count, latent_width),
        w_value[0],
        preferred_element_type=jnp.float32,
    ).astype(jnp.bfloat16)
    rows_out = jnp.dot(head_rows, out_weight, preferred_element_type=jnp.float32)
    group = lax.axis_index("grp")
    for bit_level in range(2):
        half_rows = rows_out.shape[0] // 2
        upper_side = jnp.right_shift(group, bit_level) & 1 == 1
        lower, upper = rows_out[:half_rows], rows_out[half_rows:]
        kept = jnp.where(upper_side, upper, lower)
        sent = jnp.where(upper_side, lower, upper)
        rows_out = kept + from_partner(sent.astype(jnp.bfloat16), "grp", bit_level).astype(
            jnp.float32
        )
    ring = grp_size // 4
    blocks = rows_out.reshape(ring, token_count, rows_out.shape[1])
    mine = group // 4

    def block_for(member):
        return lax.dynamic_index_in_dim(
            blocks, (member & 1) * 2 + member // 2, 0, keepdims=False
        )

    total_rows = block_for(mine)
    for step in range(1, ring):
        sent = block_for((mine + step) % ring).astype(jnp.bfloat16)
        total_rows = total_rows + shifted(sent, "grp", grp_size, 4 * step).astype(jnp.float32)
    return total_rows.astype(jnp.bfloat16)


def solution(mesh):
    return jax.shard_map(
        per_device,
        mesh=mesh,
        in_specs=(
            P(("grp", "ep"), None),
            P(("grp", "ep"), None),
            P(("grp", "ep"), None),
            P(("grp", "ep"), None, None),
            P(("grp", "ep")),
            P("grp"),
            P("grp", None),
            P(),
            P("grp", None, None),
            P("grp", None),
        ),
        out_specs=P(("grp", "ep"), None),
        check_vma=False,
    )
```

```python
import math

import jax
import jax.numpy as jnp
from jax import lax
from jax.sharding import PartitionSpec as P

TREE = 48
REQ_GRP = 4


def from_partner(block, axis, bit):
    count = lax.axis_size(axis)
    route = []
    for low in range(count):
        high = low | 1 << bit
        if high != low and high < count:
            route += [(low, high), (high, low)]
    return lax.ppermute(block, axis, route)


def shifted(block, axis, group, shift):
    count = lax.axis_size(axis)
    route = [(i, (i // group) * group + (i % group + shift) % group) for i in range(count)]
    return lax.ppermute(block, axis, route)


def bit_reversed(count):
    width = count.bit_length() - 1
    return [int(format(index, f"0{width}b")[::-1], 2) if width else 0 for index in range(count)]


def ancestors(parent_row):
    count = parent_row.shape[0]
    order = jnp.arange(count, dtype=jnp.int32)
    links = ((order[None, :] == parent_row[:, None]) & (order[:, None] > 0)).astype(jnp.float32)
    reach = jnp.eye(count, dtype=jnp.float32) + links
    for repeat in range(int(count).bit_length()):
        reach = jnp.minimum(jnp.dot(reach, reach, precision=lax.Precision.HIGHEST), 1.0)
    return reach > 0.5


def absorb(nope_rows, w_key):
    return jnp.einsum("thn,hrn->thr", nope_rows, w_key, preferred_element_type=jnp.float32).astype(
        jnp.bfloat16
    )


def append_partner(mine, partner, position, bit_level):
    upper_side = jnp.right_shift(position, bit_level) & 1 == 1
    former = jnp.where(upper_side, partner, mine)
    latter = jnp.where(upper_side, mine, partner)
    return jnp.concatenate([former, latter], axis=0)


def split_high(high):
    high_hi = high.astype(jnp.bfloat16)
    high_lo = (high - high_hi.astype(jnp.float32)).astype(jnp.bfloat16)
    return high_hi, high_lo


def pack_part(part_sum, part_high, part_total, width):
    high_hi, high_lo = split_high(part_high)
    stats = jnp.concatenate([high_hi, high_lo, part_total.astype(jnp.bfloat16)], axis=1)
    stats = jnp.pad(stats, ((0, 0), (0, width - stats.shape[1])))
    rows, heads = part_sum.shape[0], part_sum.shape[1]
    flat_sum = part_sum.astype(jnp.bfloat16).reshape(rows * heads, width)
    return jnp.concatenate([flat_sum, stats], axis=0)


def unpack_part(packed, heads):
    rows = packed.shape[0] // (heads + 1)
    stats = packed[rows * heads :].astype(jnp.float32)
    high = stats[:, :heads] + stats[:, heads : 2 * heads]
    total = stats[:, 2 * heads : 3 * heads]
    part_sum = packed[: rows * heads].reshape(rows, heads, packed.shape[1])
    return part_sum.astype(jnp.float32), high, total


def combine_parts(kept_part, received):
    kept_sum, kept_high, kept_total = kept_part
    got_sum, got_high, got_total = received
    joint_high = jnp.maximum(kept_high, got_high)
    factor_kept = jnp.exp(kept_high - joint_high)
    factor_got = jnp.exp(got_high - joint_high)
    merged_sum = kept_sum * factor_kept[..., None] + got_sum * factor_got[..., None]
    merged_total = kept_total * factor_kept + got_total * factor_got
    return (merged_sum, joint_high, merged_total)


def per_device(
    q_nope,
    q_rope,
    tree_latent,
    cache_pool,
    page_table,
    cache_len,
    parents,
    w_key,
    w_value,
    out_weight,
):
    head_count = w_key.shape[0]
    latent_width = w_key.shape[1]
    nope_width = w_key.shape[2]
    token_count = q_nope.shape[0]
    rope_width = q_rope.shape[1] // head_count
    per_request = lax.axis_size("ep") // REQ_GRP
    grp_size = lax.axis_size("grp")
    doublings = per_request.bit_length() - 1
    position = lax.axis_index("ep")
    local_rank = position % per_request
    local_request = position // per_request
    score_scale = 1.0 / math.sqrt(nope_width + rope_width)
    raw_rows = jnp.concatenate([q_nope, q_rope], axis=1)
    for bit_level in reversed(range(doublings)):
        partner = from_partner(raw_rows, "ep", bit_level)
        raw_rows = append_partner(raw_rows, partner, position, bit_level)
    nope_rows = raw_rows[:, : q_nope.shape[1]].reshape(TREE, head_count, nope_width)
    rope_rows = raw_rows[:, q_nope.shape[1] :].reshape(TREE, head_count, rope_width)
    queries = jnp.concatenate([absorb(nope_rows, w_key), rope_rows], axis=2)
    cached = cache_pool.reshape(-1, cache_pool.shape[2])
    page_count, page_rows = cache_pool.shape[0], cache_pool.shape[1]
    pos_count = cached.shape[0]
    all_keys = jnp.concatenate([cached, tree_latent], axis=0)
    slots = jnp.arange(page_count, dtype=jnp.int32)
    logical_of_slot = jnp.sum(
        jnp.where(page_table[:, None] == slots[None, :], slots[:, None], 0), axis=0
    )
    place = (
        local_rank * pos_count
        + jnp.repeat(logical_of_slot, page_rows) * page_rows
        + jnp.tile(jnp.arange(page_rows, dtype=jnp.int32), page_count)
    )
    my_length = lax.dynamic_index_in_dim(cache_len, local_request, 0, keepdims=False)
    cache_ok = place < my_length
    parent_row = lax.dynamic_index_in_dim(parents, local_request, 0, keepdims=False)
    family = ancestors(parent_row)
    tree_cols = lax.dynamic_slice_in_dim(family, local_rank * token_count, token_count, 1)
    tree_ok = tree_cols.reshape(per_request, token_count, token_count)[
        jnp.array(bit_reversed(per_request))
    ].reshape(TREE, token_count)
    allowed = jnp.concatenate(
        [jnp.broadcast_to(cache_ok[None, :], (TREE, pos_count)), tree_ok], axis=1
    )
    scores = (
        jnp.einsum("ihl,kl->ihk", queries, all_keys, preferred_element_type=jnp.float32)
        * score_scale
    )
    masked = jnp.where(allowed[:, None, :], scores, -1e30)
    highest = jnp.max(masked, axis=2)
    powers = jnp.where(allowed[:, None, :], jnp.exp(masked - highest[..., None]), 0.0)
    total = jnp.sum(powers, axis=2)
    partial_value = jnp.einsum(
        "ihk,kr->ihr",
        powers.astype(jnp.bfloat16),
        all_keys[:, :latent_width],
        preferred_element_type=jnp.float32,
    )
    state = (partial_value, highest, total)
    for bit_level in range(1):
        half_rows = state[0].shape[0] // 2
        upper_side = jnp.right_shift(position, bit_level) & 1 == 1
        lower_part = tuple((member[:half_rows] for member in state))
        upper_part = tuple((member[half_rows:] for member in state))
        kept_part = tuple(
            (jnp.where(upper_side, upper, lower) for lower, upper in zip(lower_part, upper_part))
        )
        sent_part = tuple(
            (jnp.where(upper_side, lower, upper) for lower, upper in zip(lower_part, upper_part))
        )
        received = from_partner(pack_part(*sent_part, latent_width), "ep", bit_level)
        state = combine_parts(kept_part, unpack_part(received, head_count))
    chips = per_request // 2
    chip = local_rank // 2
    chip_blocks = tuple(
        member.reshape((chips, token_count) + member.shape[1:]) for member in state
    )

    def block_of(member_chip):
        index = (member_chip & 1) * 2 + member_chip // 2
        return tuple(lax.dynamic_index_in_dim(member, index, 0, keepdims=False) for member in chip_blocks)

    parts = [block_of(chip)]
    for step in range(1, chips):
        sent = block_of((chip + step) % chips)
        got = shifted(pack_part(*sent, latent_width), "ep", per_request, 2 * step)
        parts.append(unpack_part(got, head_count))
    merged_high = parts[0][1]
    for part in parts[1:]:
        merged_high = jnp.maximum(merged_high, part[1])
    factors = [jnp.exp(part[1] - merged_high) for part in parts]
    merged_sum = sum(part[0] * factor[..., None] for part, factor in zip(parts, factors))
    merged_total = sum(part[2] * factor for part, factor in zip(parts, factors))
    merged = merged_sum / merged_total[..., None]
    spread = lax.all_to_all(
        jnp.swapaxes(merged.astype(jnp.bfloat16), 0, 1), "grp", split_axis=0, concat_axis=0, tiled=True
    )
    spread = spread.reshape(grp_size, token_count, latent_width)[jnp.array(bit_reversed(grp_size))]
    head_rows = jnp.dot(
        spread.reshape(grp_size * token_count, latent_width),
        w_value[0],
        preferred_element_type=jnp.float32,
    ).astype(jnp.bfloat16)
    rows_out = jnp.dot(head_rows, out_weight, preferred_element_type=jnp.float32)
    group = lax.axis_index("grp")
    for bit_level in range(2):
        half_rows = rows_out.shape[0] // 2
        upper_side = jnp.right_shift(group, bit_level) & 1 == 1
        lower, upper = rows_out[:half_rows], rows_out[half_rows:]
        kept = jnp.where(upper_side, upper, lower)
        sent = jnp.where(upper_side, lower, upper)
        rows_out = kept + from_partner(sent.astype(jnp.bfloat16), "grp", bit_level).astype(
            jnp.float32
        )
    ring = grp_size // 4
    blocks = rows_out.reshape(ring, token_count, rows_out.shape[1])
    mine = group // 4

    def block_for(member):
        return lax.dynamic_index_in_dim(
            blocks, (member & 1) * 2 + member // 2, 0, keepdims=False
        )

    total_rows = block_for(mine)
    for step in range(1, ring):
        sent = block_for((mine + step) % ring).astype(jnp.bfloat16)
        total_rows = total_rows + shifted(sent, "grp", grp_size, 4 * step).astype(jnp.float32)
    return total_rows.astype(jnp.bfloat16)


def solution(mesh):
    return jax.shard_map(
        per_device,
        mesh=mesh,
        in_specs=(
            P(("grp", "ep"), None),
            P(("grp", "ep"), None),
            P(("grp", "ep"), None),
            P(("grp", "ep"), None, None),
            P(("grp", "ep")),
            P("grp"),
            P("grp", None),
            P(),
            P("grp", None, None),
            P("grp", None),
        ),
        out_specs=P(("grp", "ep"), None),
        check_vma=False,
    )
```

```python
import math

import jax
import jax.numpy as jnp
from jax import lax
from jax.sharding import PartitionSpec as P

TREE = 48
REQ_GRP = 4


def from_partner(block, axis, bit):
    count = lax.axis_size(axis)
    route = []
    for low in range(count):
        high = low | 1 << bit
        if high != low and high < count:
            route += [(low, high), (high, low)]
    return lax.ppermute(block, axis, route)


def shifted(block, axis, group, shift):
    count = lax.axis_size(axis)
    route = [(i, (i // group) * group + (i % group + shift) % group) for i in range(count)]
    return lax.ppermute(block, axis, route)


def bit_reversed(count):
    width = count.bit_length() - 1
    return [int(format(index, f"0{width}b")[::-1], 2) if width else 0 for index in range(count)]


def ancestors(parent_row):
    count = parent_row.shape[0]
    order = jnp.arange(count, dtype=jnp.int32)
    links = ((order[None, :] == parent_row[:, None]) & (order[:, None] > 0)).astype(jnp.float32)
    reach = jnp.eye(count, dtype=jnp.float32) + links
    for repeat in range(int(count).bit_length()):
        reach = jnp.minimum(jnp.dot(reach, reach, precision=lax.Precision.HIGHEST), 1.0)
    return reach > 0.5


def absorb(nope_rows, w_key):
    return jnp.einsum("thn,hrn->thr", nope_rows, w_key, preferred_element_type=jnp.float32).astype(
        jnp.bfloat16
    )


def append_partner(mine, partner, position, bit_level):
    upper_side = jnp.right_shift(position, bit_level) & 1 == 1
    former = jnp.where(upper_side, partner, mine)
    latter = jnp.where(upper_side, mine, partner)
    return jnp.concatenate([former, latter], axis=0)


def split_high(high):
    high_hi = high.astype(jnp.bfloat16)
    high_lo = (high - high_hi.astype(jnp.float32)).astype(jnp.bfloat16)
    return high_hi, high_lo


def pack_part(part_sum, part_high, part_total, width):
    high_hi, high_lo = split_high(part_high)
    stats = jnp.concatenate([high_hi, high_lo, part_total.astype(jnp.bfloat16)], axis=1)
    stats = jnp.pad(stats, ((0, 0), (0, width - stats.shape[1])))
    rows, heads = part_sum.shape[0], part_sum.shape[1]
    flat_sum = part_sum.astype(jnp.bfloat16).reshape(rows * heads, width)
    return jnp.concatenate([flat_sum, stats], axis=0)


def unpack_part(packed, heads):
    rows = packed.shape[0] // (heads + 1)
    stats = packed[rows * heads :].astype(jnp.float32)
    high = stats[:, :heads] + stats[:, heads : 2 * heads]
    total = stats[:, 2 * heads : 3 * heads]
    part_sum = packed[: rows * heads].reshape(rows, heads, packed.shape[1])
    return part_sum.astype(jnp.float32), high, total


def combine_parts(kept_part, received):
    kept_sum, kept_high, kept_total = kept_part
    got_sum, got_high, got_total = received
    joint_high = jnp.maximum(kept_high, got_high)
    factor_kept = jnp.exp(kept_high - joint_high)
    factor_got = jnp.exp(got_high - joint_high)
    merged_sum = kept_sum * factor_kept[..., None] + got_sum * factor_got[..., None]
    merged_total = kept_total * factor_kept + got_total * factor_got
    return (merged_sum, joint_high, merged_total)


def per_device(
    q_nope,
    q_rope,
    tree_latent,
    cache_pool,
    page_table,
    cache_len,
    parents,
    w_key,
    w_value,
    out_weight,
):
    head_count = w_key.shape[0]
    latent_width = w_key.shape[1]
    nope_width = w_key.shape[2]
    token_count = q_nope.shape[0]
    rope_width = q_rope.shape[1] // head_count
    per_request = lax.axis_size("ep") // REQ_GRP
    grp_size = lax.axis_size("grp")
    doublings = per_request.bit_length() - 1
    position = lax.axis_index("ep")
    local_rank = position % per_request
    local_request = position // per_request
    score_scale = 1.0 / math.sqrt(nope_width + rope_width)
    raw_rows = jnp.concatenate([q_nope, q_rope], axis=1)
    for bit_level in reversed(range(doublings)):
        partner = from_partner(raw_rows, "ep", bit_level)
        raw_rows = append_partner(raw_rows, partner, position, bit_level)
    nope_rows = raw_rows[:, : q_nope.shape[1]].reshape(TREE, head_count, nope_width)
    rope_rows = raw_rows[:, q_nope.shape[1] :].reshape(TREE, head_count, rope_width)
    queries = jnp.concatenate([absorb(nope_rows, w_key), rope_rows], axis=2)
    cached = cache_pool.reshape(-1, cache_pool.shape[2])
    page_count, page_rows = cache_pool.shape[0], cache_pool.shape[1]
    pos_count = cached.shape[0]
    all_keys = jnp.concatenate([cached, tree_latent], axis=0)
    slots = jnp.arange(page_count, dtype=jnp.int32)
    logical_of_slot = jnp.sum(
        jnp.where(page_table[:, None] == slots[None, :], slots[:, None], 0), axis=0
    )
    place = (
        local_rank * pos_count
        + jnp.repeat(logical_of_slot, page_rows) * page_rows
        + jnp.tile(jnp.arange(page_rows, dtype=jnp.int32), page_count)
    )
    my_length = lax.dynamic_index_in_dim(cache_len, local_request, 0, keepdims=False)
    cache_ok = place < my_length
    parent_row = lax.dynamic_index_in_dim(parents, local_request, 0, keepdims=False)
    family = ancestors(parent_row)
    tree_cols = lax.dynamic_slice_in_dim(family, local_rank * token_count, token_count, 1)
    tree_ok = tree_cols.reshape(per_request, token_count, token_count)[
        jnp.array(bit_reversed(per_request))
    ].reshape(TREE, token_count)
    allowed = jnp.concatenate(
        [jnp.broadcast_to(cache_ok[None, :], (TREE, pos_count)), tree_ok], axis=1
    )
    scores = (
        jnp.einsum("ihl,kl->ihk", queries, all_keys, preferred_element_type=jnp.float32)
        * score_scale
    )
    masked = jnp.where(allowed[:, None, :], scores, -1e30)
    highest = jnp.max(masked, axis=2)
    powers = jnp.where(allowed[:, None, :], jnp.exp(masked - highest[..., None]), 0.0)
    total = jnp.sum(powers, axis=2)
    partial_value = jnp.einsum(
        "ihk,kr->ihr",
        powers.astype(jnp.bfloat16),
        all_keys[:, :latent_width],
        preferred_element_type=jnp.float32,
    )
    state = (partial_value, highest, total)
    for bit_level in range(doublings):
        half_rows = state[0].shape[0] // 2
        upper_side = jnp.right_shift(position, bit_level) & 1 == 1
        lower_part = tuple((member[:half_rows] for member in state))
        upper_part = tuple((member[half_rows:] for member in state))
        kept_part = tuple(
            (jnp.where(upper_side, upper, lower) for lower, upper in zip(lower_part, upper_part))
        )
        sent_part = tuple(
            (jnp.where(upper_side, lower, upper) for lower, upper in zip(lower_part, upper_part))
        )
        received = from_partner(pack_part(*sent_part, latent_width), "ep", bit_level)
        state = combine_parts(kept_part, unpack_part(received, head_count))
    merged_sum, merged_high, merged_total = state
    merged = merged_sum / merged_total[..., None]
    spread = lax.all_to_all(
        jnp.swapaxes(merged.astype(jnp.bfloat16), 0, 1), "grp", split_axis=0, concat_axis=0, tiled=True
    )
    spread = spread.reshape(grp_size, token_count, latent_width)[jnp.array(bit_reversed(grp_size))]
    head_rows = jnp.dot(
        spread.reshape(grp_size * token_count, latent_width),
        w_value[0],
        preferred_element_type=jnp.float32,
    ).astype(jnp.bfloat16)
    rows_out = jnp.dot(head_rows, out_weight, preferred_element_type=jnp.float32)
    group = lax.axis_index("grp")
    for bit_level in range(2):
        half_rows = rows_out.shape[0] // 2
        upper_side = jnp.right_shift(group, bit_level) & 1 == 1
        lower, upper = rows_out[:half_rows], rows_out[half_rows:]
        kept = jnp.where(upper_side, upper, lower)
        sent = jnp.where(upper_side, lower, upper)
        rows_out = kept + from_partner(sent.astype(jnp.bfloat16), "grp", bit_level).astype(
            jnp.float32
        )
    ring = grp_size // 4
    blocks = rows_out.reshape(ring, token_count, rows_out.shape[1])
    mine = group // 4

    def block_for(member):
        return lax.dynamic_index_in_dim(
            blocks, (member & 1) * 2 + member // 2, 0, keepdims=False
        )

    total_rows = block_for(mine)
    for step in sorted(range(1, ring), key=lambda s: -min(s, ring - s)):
        sent = block_for((mine + step) % ring).astype(jnp.bfloat16)
        total_rows = total_rows + shifted(sent, "grp", grp_size, 4 * step).astype(jnp.float32)
    return total_rows.astype(jnp.bfloat16)


def solution(mesh):
    return jax.shard_map(
        per_device,
        mesh=mesh,
        in_specs=(
            P(("grp", "ep"), None),
            P(("grp", "ep"), None),
            P(("grp", "ep"), None),
            P(("grp", "ep"), None, None),
            P(("grp", "ep")),
            P("grp"),
            P("grp", None),
            P(),
            P("grp", None, None),
            P("grp", None),
        ),
        out_specs=P(("grp", "ep"), None),
        check_vma=False,
    )
```

```python
import math

import jax
import jax.numpy as jnp
from jax import lax
from jax.sharding import PartitionSpec as P

TREE = 48
REQ_GRP = 4


def from_partner(block, axis, bit):
    count = lax.axis_size(axis)
    route = []
    for low in range(count):
        high = low | 1 << bit
        if high != low and high < count:
            route += [(low, high), (high, low)]
    return lax.ppermute(block, axis, route)


def shifted(block, axis, group, shift):
    count = lax.axis_size(axis)
    route = [(i, (i // group) * group + (i % group + shift) % group) for i in range(count)]
    return lax.ppermute(block, axis, route)


def bit_reversed(count):
    width = count.bit_length() - 1
    return [int(format(index, f"0{width}b")[::-1], 2) if width else 0 for index in range(count)]


def ancestors(parent_row):
    count = parent_row.shape[0]
    order = jnp.arange(count, dtype=jnp.int32)
    links = ((order[None, :] == parent_row[:, None]) & (order[:, None] > 0)).astype(jnp.float32)
    reach = jnp.eye(count, dtype=jnp.float32) + links
    for repeat in range(int(count).bit_length()):
        reach = jnp.minimum(jnp.dot(reach, reach, precision=lax.Precision.HIGHEST), 1.0)
    return reach > 0.5


def absorb(nope_rows, w_key):
    return jnp.einsum("thn,hrn->thr", nope_rows, w_key, preferred_element_type=jnp.float32).astype(
        jnp.bfloat16
    )


def append_partner(mine, partner, position, bit_level):
    upper_side = jnp.right_shift(position, bit_level) & 1 == 1
    former = jnp.where(upper_side, partner, mine)
    latter = jnp.where(upper_side, mine, partner)
    return jnp.concatenate([former, latter], axis=0)


def split_high(high):
    high_hi = high.astype(jnp.bfloat16)
    high_lo = (high - high_hi.astype(jnp.float32)).astype(jnp.bfloat16)
    return high_hi, high_lo


def pack_part(part_sum, part_high, part_total, width):
    high_hi, high_lo = split_high(part_high)
    stats = jnp.concatenate([high_hi, high_lo, part_total.astype(jnp.bfloat16)], axis=1)
    stats = jnp.pad(stats, ((0, 0), (0, width - stats.shape[1])))
    rows, heads = part_sum.shape[0], part_sum.shape[1]
    flat_sum = part_sum.astype(jnp.bfloat16).reshape(rows * heads, width)
    return jnp.concatenate([flat_sum, stats], axis=0)


def unpack_part(packed, heads):
    rows = packed.shape[0] // (heads + 1)
    stats = packed[rows * heads :].astype(jnp.float32)
    high = stats[:, :heads] + stats[:, heads : 2 * heads]
    total = stats[:, 2 * heads : 3 * heads]
    part_sum = packed[: rows * heads].reshape(rows, heads, packed.shape[1])
    return part_sum.astype(jnp.float32), high, total


def combine_parts(kept_part, received):
    kept_sum, kept_high, kept_total = kept_part
    got_sum, got_high, got_total = received
    joint_high = jnp.maximum(kept_high, got_high)
    factor_kept = jnp.exp(kept_high - joint_high)
    factor_got = jnp.exp(got_high - joint_high)
    merged_sum = kept_sum * factor_kept[..., None] + got_sum * factor_got[..., None]
    merged_total = kept_total * factor_kept + got_total * factor_got
    return (merged_sum, joint_high, merged_total)


def per_device(
    q_nope,
    q_rope,
    tree_latent,
    cache_pool,
    page_table,
    cache_len,
    parents,
    w_key,
    w_value,
    out_weight,
):
    head_count = w_key.shape[0]
    latent_width = w_key.shape[1]
    nope_width = w_key.shape[2]
    token_count = q_nope.shape[0]
    rope_width = q_rope.shape[1] // head_count
    per_request = lax.axis_size("ep") // REQ_GRP
    grp_size = lax.axis_size("grp")
    doublings = per_request.bit_length() - 1
    position = lax.axis_index("ep")
    local_rank = position % per_request
    local_request = position // per_request
    score_scale = 1.0 / math.sqrt(nope_width + rope_width)
    raw_rows = jnp.concatenate([q_nope, q_rope], axis=1)
    for bit_level in reversed(range(doublings)):
        partner = from_partner(raw_rows, "ep", bit_level)
        raw_rows = append_partner(raw_rows, partner, position, bit_level)
    nope_rows = raw_rows[:, : q_nope.shape[1]].reshape(TREE, head_count, nope_width)
    rope_rows = raw_rows[:, q_nope.shape[1] :].reshape(TREE, head_count, rope_width)
    queries = jnp.concatenate([absorb(nope_rows, w_key), rope_rows], axis=2)
    cached = cache_pool.reshape(-1, cache_pool.shape[2])
    page_count, page_rows = cache_pool.shape[0], cache_pool.shape[1]
    pos_count = cached.shape[0]
    all_keys = jnp.concatenate([cached, tree_latent], axis=0)
    slots = jnp.arange(page_count, dtype=jnp.int32)
    logical_of_slot = jnp.sum(
        jnp.where(page_table[:, None] == slots[None, :], slots[:, None], 0), axis=0
    )
    place = (
        local_rank * pos_count
        + jnp.repeat(logical_of_slot, page_rows) * page_rows
        + jnp.tile(jnp.arange(page_rows, dtype=jnp.int32), page_count)
    )
    my_length = lax.dynamic_index_in_dim(cache_len, local_request, 0, keepdims=False)
    cache_ok = place < my_length
    parent_row = lax.dynamic_index_in_dim(parents, local_request, 0, keepdims=False)
    family = ancestors(parent_row)
    tree_cols = lax.dynamic_slice_in_dim(family, local_rank * token_count, token_count, 1)
    tree_ok = tree_cols.reshape(per_request, token_count, token_count)[
        jnp.array(bit_reversed(per_request))
    ].reshape(TREE, token_count)
    allowed = jnp.concatenate(
        [jnp.broadcast_to(cache_ok[None, :], (TREE, pos_count)), tree_ok], axis=1
    )
    scores = (
        jnp.einsum("ihl,kl->ihk", queries, all_keys, preferred_element_type=jnp.float32)
        * score_scale
    )
    masked = jnp.where(allowed[:, None, :], scores, -1e30)
    highest = jnp.max(masked, axis=2)
    powers = jnp.where(allowed[:, None, :], jnp.exp(masked - highest[..., None]), 0.0)
    total = jnp.sum(powers, axis=2)
    partial_value = jnp.einsum(
        "ihk,kr->ihr",
        powers.astype(jnp.bfloat16),
        all_keys[:, :latent_width],
        preferred_element_type=jnp.float32,
    )
    state = (partial_value, highest, total)
    for bit_level in range(1):
        half_rows = state[0].shape[0] // 2
        upper_side = jnp.right_shift(position, bit_level) & 1 == 1
        lower_part = tuple((member[:half_rows] for member in state))
        upper_part = tuple((member[half_rows:] for member in state))
        kept_part = tuple(
            (jnp.where(upper_side, upper, lower) for lower, upper in zip(lower_part, upper_part))
        )
        sent_part = tuple(
            (jnp.where(upper_side, lower, upper) for lower, upper in zip(lower_part, upper_part))
        )
        received = from_partner(pack_part(*sent_part, latent_width), "ep", bit_level)
        state = combine_parts(kept_part, unpack_part(received, head_count))
    chips = per_request // 2
    chip = local_rank // 2
    chip_blocks = tuple(
        member.reshape((chips, token_count) + member.shape[1:]) for member in state
    )

    def block_of(member_chip):
        index = (member_chip & 1) * 2 + member_chip // 2
        return tuple(lax.dynamic_index_in_dim(member, index, 0, keepdims=False) for member in chip_blocks)

    parts = [block_of(chip)]
    far_step = chips // 2
    far_packet = pack_part(*block_of((chip + far_step) % chips), latent_width)
    far_packet, chip_blocks = lax.optimization_barrier((far_packet, chip_blocks))
    parts.append(unpack_part(shifted(far_packet, "ep", per_request, 2 * far_step), head_count))
    for step in range(1, chips):
        if step == far_step:
            continue
        sent = block_of((chip + step) % chips)
        got = shifted(pack_part(*sent, latent_width), "ep", per_request, 2 * step)
        parts.append(unpack_part(got, head_count))
    merged_high = parts[0][1]
    for part in parts[1:]:
        merged_high = jnp.maximum(merged_high, part[1])
    factors = [jnp.exp(part[1] - merged_high) for part in parts]
    merged_sum = sum(part[0] * factor[..., None] for part, factor in zip(parts, factors))
    merged_total = sum(part[2] * factor for part, factor in zip(parts, factors))
    merged = merged_sum / merged_total[..., None]
    spread = lax.all_to_all(
        jnp.swapaxes(merged.astype(jnp.bfloat16), 0, 1), "grp", split_axis=0, concat_axis=0, tiled=True
    )
    spread = spread.reshape(grp_size, token_count, latent_width)[jnp.array(bit_reversed(grp_size))]
    head_rows = jnp.dot(
        spread.reshape(grp_size * token_count, latent_width),
        w_value[0],
        preferred_element_type=jnp.float32,
    ).astype(jnp.bfloat16)
    rows_out = jnp.dot(head_rows, out_weight, preferred_element_type=jnp.float32)
    group = lax.axis_index("grp")
    for bit_level in range(2):
        half_rows = rows_out.shape[0] // 2
        upper_side = jnp.right_shift(group, bit_level) & 1 == 1
        lower, upper = rows_out[:half_rows], rows_out[half_rows:]
        kept = jnp.where(upper_side, upper, lower)
        sent = jnp.where(upper_side, lower, upper)
        rows_out = kept + from_partner(sent.astype(jnp.bfloat16), "grp", bit_level).astype(
            jnp.float32
        )
    ring = grp_size // 4
    blocks = rows_out.reshape(ring, token_count, rows_out.shape[1])
    mine = group // 4

    def block_for(member):
        return lax.dynamic_index_in_dim(
            blocks, (member & 1) * 2 + member // 2, 0, keepdims=False
        )

    total_rows = block_for(mine)
    for step in sorted(range(1, ring), key=lambda s: -min(s, ring - s)):
        sent = block_for((mine + step) % ring).astype(jnp.bfloat16)
        total_rows = total_rows + shifted(sent, "grp", grp_size, 4 * step).astype(jnp.float32)
    return total_rows.astype(jnp.bfloat16)


def solution(mesh):
    return jax.shard_map(
        per_device,
        mesh=mesh,
        in_specs=(
            P(("grp", "ep"), None),
            P(("grp", "ep"), None),
            P(("grp", "ep"), None),
            P(("grp", "ep"), None, None),
            P(("grp", "ep")),
            P("grp"),
            P("grp", None),
            P(),
            P("grp", None, None),
            P("grp", None),
        ),
        out_specs=P(("grp", "ep"), None),
        check_vma=False,
    )
```

```python
import math

import jax
import jax.numpy as jnp
from jax import lax
from jax.sharding import PartitionSpec as P

TREE = 48
REQ_GRP = 4


def from_partner(block, axis, bit):
    count = lax.axis_size(axis)
    route = []
    for low in range(count):
        high = low | 1 << bit
        if high != low and high < count:
            route += [(low, high), (high, low)]
    return lax.ppermute(block, axis, route)


def shifted(block, axis, group, shift):
    count = lax.axis_size(axis)
    route = [(i, (i // group) * group + (i % group + shift) % group) for i in range(count)]
    return lax.ppermute(block, axis, route)


def bit_reversed(count):
    width = count.bit_length() - 1
    return [int(format(index, f"0{width}b")[::-1], 2) if width else 0 for index in range(count)]


def ancestors(parent_row):
    count = parent_row.shape[0]
    order = jnp.arange(count, dtype=jnp.int32)
    links = ((order[None, :] == parent_row[:, None]) & (order[:, None] > 0)).astype(jnp.float32)
    reach = jnp.eye(count, dtype=jnp.float32) + links
    for repeat in range(int(count).bit_length()):
        reach = jnp.minimum(jnp.dot(reach, reach, precision=lax.Precision.HIGHEST), 1.0)
    return reach > 0.5


def absorb(nope_rows, w_key):
    return jnp.einsum("thn,hrn->thr", nope_rows, w_key, preferred_element_type=jnp.float32).astype(
        jnp.bfloat16
    )


def append_partner(mine, partner, position, bit_level):
    upper_side = jnp.right_shift(position, bit_level) & 1 == 1
    former = jnp.where(upper_side, partner, mine)
    latter = jnp.where(upper_side, mine, partner)
    return jnp.concatenate([former, latter], axis=0)


def split_high(high):
    high_hi = high.astype(jnp.bfloat16)
    high_lo = (high - high_hi.astype(jnp.float32)).astype(jnp.bfloat16)
    return high_hi, high_lo


def pack_part(part_sum, part_high, part_total, width):
    high_hi, high_lo = split_high(part_high)
    stats = jnp.concatenate([high_hi, high_lo, part_total.astype(jnp.bfloat16)], axis=1)
    stats = jnp.pad(stats, ((0, 0), (0, width - stats.shape[1])))
    rows, heads = part_sum.shape[0], part_sum.shape[1]
    flat_sum = part_sum.astype(jnp.bfloat16).reshape(rows * heads, width)
    return jnp.concatenate([flat_sum, stats], axis=0)


def unpack_part(packed, heads):
    rows = packed.shape[0] // (heads + 1)
    stats = packed[rows * heads :].astype(jnp.float32)
    high = stats[:, :heads] + stats[:, heads : 2 * heads]
    total = stats[:, 2 * heads : 3 * heads]
    part_sum = packed[: rows * heads].reshape(rows, heads, packed.shape[1])
    return part_sum.astype(jnp.float32), high, total


def combine_parts(kept_part, received):
    kept_sum, kept_high, kept_total = kept_part
    got_sum, got_high, got_total = received
    joint_high = jnp.maximum(kept_high, got_high)
    factor_kept = jnp.exp(kept_high - joint_high)
    factor_got = jnp.exp(got_high - joint_high)
    merged_sum = kept_sum * factor_kept[..., None] + got_sum * factor_got[..., None]
    merged_total = kept_total * factor_kept + got_total * factor_got
    return (merged_sum, joint_high, merged_total)


def per_device(
    q_nope,
    q_rope,
    tree_latent,
    cache_pool,
    page_table,
    cache_len,
    parents,
    w_key,
    w_value,
    out_weight,
):
    head_count = w_key.shape[0]
    latent_width = w_key.shape[1]
    nope_width = w_key.shape[2]
    token_count = q_nope.shape[0]
    rope_width = q_rope.shape[1] // head_count
    per_request = lax.axis_size("ep") // REQ_GRP
    grp_size = lax.axis_size("grp")
    doublings = per_request.bit_length() - 1
    position = lax.axis_index("ep")
    local_rank = position % per_request
    local_request = position // per_request
    score_scale = 1.0 / math.sqrt(nope_width + rope_width)
    raw_rows = jnp.concatenate([q_nope, q_rope], axis=1)
    for bit_level in reversed(range(doublings)):
        partner = from_partner(raw_rows, "ep", bit_level)
        raw_rows = append_partner(raw_rows, partner, position, bit_level)
    nope_rows = raw_rows[:, : q_nope.shape[1]].reshape(TREE, head_count, nope_width)
    rope_rows = raw_rows[:, q_nope.shape[1] :].reshape(TREE, head_count, rope_width)
    queries = jnp.concatenate([absorb(nope_rows, w_key), rope_rows], axis=2)
    cached = cache_pool.reshape(-1, cache_pool.shape[2])
    page_count, page_rows = cache_pool.shape[0], cache_pool.shape[1]
    pos_count = cached.shape[0]
    all_keys = jnp.concatenate([cached, tree_latent], axis=0)
    slots = jnp.arange(page_count, dtype=jnp.int32)
    logical_of_slot = jnp.sum(
        jnp.where(page_table[:, None] == slots[None, :], slots[:, None], 0), axis=0
    )
    place = (
        local_rank * pos_count
        + jnp.repeat(logical_of_slot, page_rows) * page_rows
        + jnp.tile(jnp.arange(page_rows, dtype=jnp.int32), page_count)
    )
    my_length = lax.dynamic_index_in_dim(cache_len, local_request, 0, keepdims=False)
    cache_ok = place < my_length
    parent_row = lax.dynamic_index_in_dim(parents, local_request, 0, keepdims=False)
    family = ancestors(parent_row)
    tree_cols = lax.dynamic_slice_in_dim(family, local_rank * token_count, token_count, 1)
    tree_ok = tree_cols.reshape(per_request, token_count, token_count)[
        jnp.array(bit_reversed(per_request))
    ].reshape(TREE, token_count)
    allowed = jnp.concatenate(
        [jnp.broadcast_to(cache_ok[None, :], (TREE, pos_count)), tree_ok], axis=1
    )
    scores = (
        jnp.einsum("ihl,kl->ihk", queries, all_keys, preferred_element_type=jnp.float32)
        * score_scale
    )
    masked = jnp.where(allowed[:, None, :], scores, -1e30)
    highest = jnp.max(masked, axis=2)
    powers = jnp.where(allowed[:, None, :], jnp.exp(masked - highest[..., None]), 0.0)
    total = jnp.sum(powers, axis=2)
    partial_value = jnp.einsum(
        "ihk,kr->ihr",
        powers.astype(jnp.bfloat16),
        all_keys[:, :latent_width],
        preferred_element_type=jnp.float32,
    )
    state = (partial_value, highest, total)
    for bit_level in range(doublings):
        half_rows = state[0].shape[0] // 2
        upper_side = jnp.right_shift(position, bit_level) & 1 == 1
        lower_part = tuple((member[:half_rows] for member in state))
        upper_part = tuple((member[half_rows:] for member in state))
        kept_part = tuple(
            (jnp.where(upper_side, upper, lower) for lower, upper in zip(lower_part, upper_part))
        )
        sent_part = tuple(
            (jnp.where(upper_side, lower, upper) for lower, upper in zip(lower_part, upper_part))
        )
        received = from_partner(pack_part(*sent_part, latent_width), "ep", bit_level)
        state = combine_parts(kept_part, unpack_part(received, head_count))
    merged_sum, merged_high, merged_total = state
    merged = merged_sum / merged_total[..., None]
    spread = lax.all_to_all(
        jnp.swapaxes(merged.astype(jnp.bfloat16), 0, 1), "grp", split_axis=0, concat_axis=0, tiled=True
    )
    spread = spread.reshape(grp_size, token_count, latent_width)[jnp.array(bit_reversed(grp_size))]
    head_rows = jnp.dot(
        spread.reshape(grp_size * token_count, latent_width),
        w_value[0],
        preferred_element_type=jnp.float32,
    ).astype(jnp.bfloat16)
    rows_out = jnp.dot(head_rows, out_weight, preferred_element_type=jnp.float32)
    group = lax.axis_index("grp")
    for bit_level in range(2):
        half_rows = rows_out.shape[0] // 2
        upper_side = jnp.right_shift(group, bit_level) & 1 == 1
        lower, upper = rows_out[:half_rows], rows_out[half_rows:]
        kept = jnp.where(upper_side, upper, lower)
        sent = jnp.where(upper_side, lower, upper)
        rows_out = kept + from_partner(sent.astype(jnp.bfloat16), "grp", bit_level).astype(
            jnp.float32
        )
    ring = grp_size // 4
    blocks = rows_out.reshape(ring, token_count, rows_out.shape[1])
    mine = group // 4

    def block_for(member):
        return lax.dynamic_index_in_dim(
            blocks, (member & 1) * 2 + member // 2, 0, keepdims=False
        )

    total_rows = block_for(mine)
    for step in sorted(range(1, ring), key=lambda s: (-min(s, ring - s), -s)):
        sent = block_for((mine + step) % ring).astype(jnp.bfloat16)
        total_rows = total_rows + shifted(sent, "grp", grp_size, 4 * step).astype(jnp.float32)
    return total_rows.astype(jnp.bfloat16)


def solution(mesh):
    return jax.shard_map(
        per_device,
        mesh=mesh,
        in_specs=(
            P(("grp", "ep"), None),
            P(("grp", "ep"), None),
            P(("grp", "ep"), None),
            P(("grp", "ep"), None, None),
            P(("grp", "ep")),
            P("grp"),
            P("grp", None),
            P(),
            P("grp", None, None),
            P("grp", None),
        ),
        out_specs=P(("grp", "ep"), None),
        check_vma=False,
    )
```

```python
import math

import jax
import jax.numpy as jnp
from jax import lax
from jax.sharding import PartitionSpec as P

TREE = 48
REQ_GRP = 4


def from_partner(block, axis, bit):
    count = lax.axis_size(axis)
    route = []
    for low in range(count):
        high = low | 1 << bit
        if high != low and high < count:
            route += [(low, high), (high, low)]
    return lax.ppermute(block, axis, route)


def shifted(block, axis, group, shift):
    count = lax.axis_size(axis)
    route = [(i, (i // group) * group + (i % group + shift) % group) for i in range(count)]
    return lax.ppermute(block, axis, route)


def bit_reversed(count):
    width = count.bit_length() - 1
    return [int(format(index, f"0{width}b")[::-1], 2) if width else 0 for index in range(count)]


def ancestors(parent_row):
    count = parent_row.shape[0]
    order = jnp.arange(count, dtype=jnp.int32)
    links = ((order[None, :] == parent_row[:, None]) & (order[:, None] > 0)).astype(jnp.float32)
    reach = jnp.eye(count, dtype=jnp.float32) + links
    for repeat in range(int(count).bit_length()):
        reach = jnp.minimum(jnp.dot(reach, reach, precision=lax.Precision.HIGHEST), 1.0)
    return reach > 0.5


def absorb(nope_rows, w_key):
    return jnp.einsum("thn,hrn->thr", nope_rows, w_key, preferred_element_type=jnp.float32).astype(
        jnp.bfloat16
    )


def append_partner(mine, partner, position, bit_level):
    upper_side = jnp.right_shift(position, bit_level) & 1 == 1
    former = jnp.where(upper_side, partner, mine)
    latter = jnp.where(upper_side, mine, partner)
    return jnp.concatenate([former, latter], axis=0)


def split_high(high):
    high_hi = high.astype(jnp.bfloat16)
    high_lo = (high - high_hi.astype(jnp.float32)).astype(jnp.bfloat16)
    return high_hi, high_lo


def pack_part(part_sum, part_high, part_total, width):
    high_hi, high_lo = split_high(part_high)
    stats = jnp.concatenate([high_hi, high_lo, part_total.astype(jnp.bfloat16)], axis=1)
    stats = jnp.pad(stats, ((0, 0), (0, width - stats.shape[1])))
    rows, heads = part_sum.shape[0], part_sum.shape[1]
    flat_sum = part_sum.astype(jnp.bfloat16).reshape(rows * heads, width)
    return jnp.concatenate([flat_sum, stats], axis=0)


def unpack_part(packed, heads):
    rows = packed.shape[0] // (heads + 1)
    stats = packed[rows * heads :].astype(jnp.float32)
    high = stats[:, :heads] + stats[:, heads : 2 * heads]
    total = stats[:, 2 * heads : 3 * heads]
    part_sum = packed[: rows * heads].reshape(rows, heads, packed.shape[1])
    return part_sum.astype(jnp.float32), high, total


def combine_parts(kept_part, received):
    kept_sum, kept_high, kept_total = kept_part
    got_sum, got_high, got_total = received
    joint_high = jnp.maximum(kept_high, got_high)
    factor_kept = jnp.exp(kept_high - joint_high)
    factor_got = jnp.exp(got_high - joint_high)
    merged_sum = kept_sum * factor_kept[..., None] + got_sum * factor_got[..., None]
    merged_total = kept_total * factor_kept + got_total * factor_got
    return (merged_sum, joint_high, merged_total)


def per_device(
    q_nope,
    q_rope,
    tree_latent,
    cache_pool,
    page_table,
    cache_len,
    parents,
    w_key,
    w_value,
    out_weight,
):
    head_count = w_key.shape[0]
    latent_width = w_key.shape[1]
    nope_width = w_key.shape[2]
    token_count = q_nope.shape[0]
    rope_width = q_rope.shape[1] // head_count
    per_request = lax.axis_size("ep") // REQ_GRP
    grp_size = lax.axis_size("grp")
    doublings = per_request.bit_length() - 1
    position = lax.axis_index("ep")
    local_rank = position % per_request
    local_request = position // per_request
    score_scale = 1.0 / math.sqrt(nope_width + rope_width)
    nope_cols, rope_cols = q_nope.shape[1], q_rope.shape[1]
    raw_rows = jnp.pad(q_nope, ((0, 0), (0, rope_cols))) + jnp.pad(q_rope, ((0, 0), (nope_cols, 0)))
    for bit_level in reversed(range(doublings)):
        partner = from_partner(raw_rows, "ep", bit_level)
        raw_rows = append_partner(raw_rows, partner, position, bit_level)
    nope_rows = raw_rows[:, : q_nope.shape[1]].reshape(TREE, head_count, nope_width)
    rope_rows = raw_rows[:, q_nope.shape[1] :].reshape(TREE, head_count, rope_width)
    queries = jnp.concatenate([absorb(nope_rows, w_key), rope_rows], axis=2)
    cached = cache_pool.reshape(-1, cache_pool.shape[2])
    page_count, page_rows = cache_pool.shape[0], cache_pool.shape[1]
    pos_count = cached.shape[0]
    all_keys = jnp.concatenate([cached, tree_latent], axis=0)
    slots = jnp.arange(page_count, dtype=jnp.int32)
    logical_of_slot = jnp.sum(
        jnp.where(page_table[:, None] == slots[None, :], slots[:, None], 0), axis=0
    )
    place = (
        local_rank * pos_count
        + jnp.repeat(logical_of_slot, page_rows) * page_rows
        + jnp.tile(jnp.arange(page_rows, dtype=jnp.int32), page_count)
    )
    my_length = lax.dynamic_index_in_dim(cache_len, local_request, 0, keepdims=False)
    cache_ok = place < my_length
    parent_row = lax.dynamic_index_in_dim(parents, local_request, 0, keepdims=False)
    family = ancestors(parent_row)
    tree_cols = lax.dynamic_slice_in_dim(family, local_rank * token_count, token_count, 1)
    tree_ok = tree_cols.reshape(per_request, token_count, token_count)[
        jnp.array(bit_reversed(per_request))
    ].reshape(TREE, token_count)
    allowed = jnp.concatenate(
        [jnp.broadcast_to(cache_ok[None, :], (TREE, pos_count)), tree_ok], axis=1
    )
    scores = (
        jnp.einsum("ihl,kl->ihk", queries, all_keys, preferred_element_type=jnp.float32)
        * score_scale
    )
    masked = jnp.where(allowed[:, None, :], scores, -1e30)
    highest = jnp.max(masked, axis=2)
    powers = jnp.where(allowed[:, None, :], jnp.exp(masked - highest[..., None]), 0.0)
    total = jnp.sum(powers, axis=2)
    partial_value = jnp.einsum(
        "ihk,kr->ihr",
        powers.astype(jnp.bfloat16),
        all_keys[:, :latent_width],
        preferred_element_type=jnp.float32,
    )
    state = (partial_value, highest, total)
    for bit_level in range(doublings):
        half_rows = state[0].shape[0] // 2
        upper_side = jnp.right_shift(position, bit_level) & 1 == 1
        lower_part = tuple((member[:half_rows] for member in state))
        upper_part = tuple((member[half_rows:] for member in state))
        kept_part = tuple(
            (jnp.where(upper_side, upper, lower) for lower, upper in zip(lower_part, upper_part))
        )
        sent_part = tuple(
            (jnp.where(upper_side, lower, upper) for lower, upper in zip(lower_part, upper_part))
        )
        received = from_partner(pack_part(*sent_part, latent_width), "ep", bit_level)
        state = combine_parts(kept_part, unpack_part(received, head_count))
    merged_sum, merged_high, merged_total = state
    merged = merged_sum / merged_total[..., None]
    spread = lax.all_to_all(
        jnp.swapaxes(merged.astype(jnp.bfloat16), 0, 1), "grp", split_axis=0, concat_axis=0, tiled=True
    )
    spread = spread.reshape(grp_size, token_count, latent_width)[jnp.array(bit_reversed(grp_size))]
    head_rows = jnp.dot(
        spread.reshape(grp_size * token_count, latent_width),
        w_value[0],
        preferred_element_type=jnp.float32,
    ).astype(jnp.bfloat16)
    rows_out = jnp.dot(head_rows, out_weight, preferred_element_type=jnp.float32)
    group = lax.axis_index("grp")
    for bit_level in range(2):
        half_rows = rows_out.shape[0] // 2
        upper_side = jnp.right_shift(group, bit_level) & 1 == 1
        lower, upper = rows_out[:half_rows], rows_out[half_rows:]
        kept = jnp.where(upper_side, upper, lower)
        sent = jnp.where(upper_side, lower, upper)
        rows_out = kept + from_partner(sent.astype(jnp.bfloat16), "grp", bit_level).astype(
            jnp.float32
        )
    ring = grp_size // 4
    blocks = rows_out.reshape(ring, token_count, rows_out.shape[1])
    mine = group // 4

    def block_for(member):
        return lax.dynamic_index_in_dim(
            blocks, (member & 1) * 2 + member // 2, 0, keepdims=False
        )

    total_rows = block_for(mine)
    for step in sorted(range(1, ring), key=lambda s: (-min(s, ring - s), -s)):
        sent = block_for((mine + step) % ring).astype(jnp.bfloat16)
        total_rows = total_rows + shifted(sent, "grp", grp_size, 4 * step).astype(jnp.float32)
    return total_rows.astype(jnp.bfloat16)


def solution(mesh):
    return jax.shard_map(
        per_device,
        mesh=mesh,
        in_specs=(
            P(("grp", "ep"), None),
            P(("grp", "ep"), None),
            P(("grp", "ep"), None),
            P(("grp", "ep"), None, None),
            P(("grp", "ep")),
            P("grp"),
            P("grp", None),
            P(),
            P("grp", None, None),
            P("grp", None),
        ),
        out_specs=P(("grp", "ep"), None),
        check_vma=False,
    )
```
